128 devices in a mesh: gx: 16 (over z, x), gy: 8 (over y, core).
Axes of the slice: x: 4, y: 4, z: 4, core: 2. Of those that a mesh axis runs over, the one named last changes fastest.
Arguments:
- velocity: float32 [3, 128, 128, 128], P(None, 'gx', 'gy'), may hold values from -6 to 6
- stress: float32 [6, 128, 128, 128], P(None, 'gx', 'gy'), may hold values from -6 to 6
- lame_first: float32 [128, 128, 128], P('gx', 'gy'), may hold values from 0.5 to 1.5
- shear_modulus: float32 [128, 128, 128], P('gx', 'gy'), may hold values from 0.3 to 1
- buoyancy: float32 [128, 128, 128], P('gx', 'gy'), may hold values from 0.5 to 1
- forward_strain: bfloat16 [12, 128, 128, 128], P(None, 'gx', 'gy'), may hold values from -6 to 6
- lame_accum: float32 [128, 128, 128], P('gx', 'gy'), may hold values from -6 to 6
- shear_accum: float32 [128, 128, 128], P('gx', 'gy'), may hold values from -6 to 6
- residuals: bfloat16 [4096, 4096], P(('gx', 'gy')), may hold values from -24 to 24
- station_cell: int32 [4096], P(('gx', 'gy')), may hold values from 0 to 127
- station_pairs: int32 [16384, 2], replicated, may hold values from 0 to 4095, as said below
Outputs:
- new_velocity: float32 [3, 128, 128, 128], P(None, 'gx', 'gy')
- new_stress: float32 [6, 128, 128, 128], P(None, 'gx', 'gy')
- lame_kernel: float32 [128, 128, 128], P('gx', 'gy')
- shear_kernel: float32 [128, 128, 128], P('gx', 'gy')
- adjoint_source: float32 [4096, 4096], P(('gx', 'gy'))
The draws below stay inside these ranges and needn't reach their ends.
Inputs may be any that keep to these rules, and one draw needn't show every extreme that they name: station_cell[s] numbers the surface cell x * 16 + y of station s within the block of the device that holds station s. `station_pairs`: stations s * 32 to (s + 1) * 32 - 1 are held by device s of gx+gy. The first station of pair p is held by device p // 128. Among the 128 pairs of one device, at most 2 have a second station held by any one device; some may have none. Some device's stations are the second station of exactly 2 pairs of every device.
All inputs are finite; a program needn't handle non-finite values.
Results may differ from the reference program's by a relative error of at most 0.0017.
Values may be sent and summed in bfloat16 or wider, within the bound.
No kernel may reach another device: no remote copies, remote signals or barrier semaphores. Data moves between devices by JAX's collectives and lax.ppermute only.
A program may use at most 64 MiB of HBM per device.

```python
import math
import jax
import jax.numpy as jnp
from jax import lax

CX = 8
CY = 16
NSAMP = 4096
STEPS = 2
STA_DEV = 32
P_DEV = 128
NX = 128
NY = 128
NZ = 128
STATIONS = 4096
PAIRS = 16384
CAP = 2
SLOTS = 256
N_GY = 8


def draw_residuals(key, part):
    common = jnp.clip(jax.random.normal(jax.random.fold_in(key, 21), (NSAMP,), jnp.float32), -4.0, 4.0)
    mixing = jax.random.uniform(jax.random.fold_in(key, 22), (STATIONS, 1), jnp.float32, 0.0, 1.5)
    own_part = jnp.clip(jax.random.normal(jax.random.fold_in(key, 23), (STATIONS, NSAMP), jnp.float32), -4.0, 4.0)
    station_gain = jnp.exp(jax.random.uniform(jax.random.fold_in(key, 24), (STATIONS, 1), jnp.float32, math.log(0.3), math.log(3.0)))
    return (station_gain * (0.7 * mixing * common[None, :] + 0.7 * own_part)).astype(jnp.bfloat16)


def draw_station_pairs(key, part):
    devices = PAIRS // P_DEV
    owner_level = jax.random.randint(jax.random.fold_in(key, 11), (devices,), 0, 3)
    hottest = jax.random.randint(jax.random.fold_in(key, 12), (), 0, devices)
    slot_owner = jnp.arange(SLOTS) // CAP

    def one_device(device_number):
        device_key = jax.random.fold_in(key, 1000 + device_number)
        ranking = jax.random.permutation(jax.random.fold_in(device_key, 1), SLOTS)
        slot_score = jnp.where(slot_owner == hottest, ranking - SLOTS, owner_level[slot_owner] * SLOTS + ranking)
        chosen = jnp.argsort(slot_score, stable=True)[:P_DEV]
        owners = chosen // CAP
        second_station = owners * STA_DEV + jax.random.randint(jax.random.fold_in(device_key, 2), (P_DEV,), 0, STA_DEV)
        first_station = device_number * STA_DEV + jax.random.randint(jax.random.fold_in(device_key, 3), (P_DEV,), 0, STA_DEV)
        return jnp.stack([first_station, second_station], axis=1)
    return jax.vmap(one_device)(jnp.arange(devices)).reshape(PAIRS, 2).astype(jnp.int32)


def plant(result, own_key, least, high):
    longest = result.shape.index(max(result.shape))
    spots = []
    for shift in (0, 1):
        where = [jax.random.randint(jax.random.fold_in(own_key, axis), (), 0, length) for axis, length in enumerate(result.shape)]
        where[longest] = (where[longest] + shift) % result.shape[longest]
        spots.append(tuple(where))
    return result.at[spots[0]].set(least).at[spots[1]].set(high)


def levels(rng, shape, shards, low, top_value):
    def one(dim, shards_of):
        draws = jax.random.uniform(jax.random.fold_in(jax.random.fold_in(rng, 6), dim), (shards_of,), jnp.float32, low / len(shards), top_value / len(shards))
        return jnp.repeat(jnp.exp(draws), shape[dim] // shards_of).reshape((-1,) + (1,) * (len(shape) - dim - 1))

    factor_of = one(*shards[0])
    for cut in shards[1:]:
        factor_of = factor_of * one(*cut)
    return factor_of


def noise(own_key, shape, scale, limit, shards=(), kind=jnp.bfloat16):
    result = scale * jax.random.normal(own_key, shape, jnp.float32)
    if shards:
        result = result * levels(own_key, shape, shards, -0.22, 0.18)
    return jnp.clip(result, -limit, limit).astype(kind)


def setup_inputs(seed: int = 0) -> dict:
    keys = jax.random.split(jax.random.key(seed), 12)
    return {
        "velocity": noise(keys[0], (3, NX, NY, NZ), 1.0, 6.0, ((1, 16), (2, 8)), jnp.float32),
        "stress": noise(keys[1], (6, NX, NY, NZ), 1.0, 6.0, ((1, 16), (2, 8)), jnp.float32),
        "lame_first": jnp.clip(jnp.exp(math.log(1.5) - 1.0986123 * jax.random.uniform(keys[2], (NX, NY, NZ), jnp.float32) ** levels(keys[2], (NX, NY, NZ), ((0, 16), (1, 8)), -0.2, 0.2)), 0.5, 1.5),
        "shear_modulus": jnp.clip(jnp.exp(math.log(1.0) - 1.2039728 * jax.random.uniform(keys[3], (NX, NY, NZ), jnp.float32) ** levels(keys[3], (NX, NY, NZ), ((0, 16), (1, 8)), -0.2, 0.2)), 0.3, 1.0),
        "buoyancy": jnp.clip(jnp.exp(math.log(1.0) - 0.6931472 * jax.random.uniform(keys[4], (NX, NY, NZ), jnp.float32) ** levels(keys[4], (NX, NY, NZ), ((0, 16), (1, 8)), -0.2, 0.2)), 0.5, 1.0),
        "forward_strain": noise(keys[5], (STEPS * 6, NX, NY, NZ), 1.0, 6.0, ((1, 16), (2, 8))),
        "lame_accum": noise(keys[6], (NX, NY, NZ), 1.0, 6.0, ((0, 16), (1, 8)), jnp.float32),
        "shear_accum": noise(keys[7], (NX, NY, NZ), 1.0, 6.0, ((0, 16), (1, 8)), jnp.float32),
        "residuals": draw_residuals(jax.random.fold_in(keys[11], 71), 0),
        "station_cell": plant(jax.random.randint(keys[9], (STATIONS,), 0, CX * CY), jax.random.fold_in(keys[9], 1), 0, (CX * CY) - 1).astype(jnp.int32),
        "station_pairs": draw_station_pairs(jax.random.fold_in(keys[11], 71), 0),
    }


near_weight = 9.0 / 8.0
far_weight = -1.0 / 24.0
time_step = 0.25
epsilon = 1e-06

def shifted(padded, start, length, axis):
    return lax.slice_in_dim(padded, start, start + length, axis=axis)

def backward_diff(padded, length, axis):
    return near_weight * (shifted(padded, 2, length, axis) - shifted(padded, 1, length, axis)) + far_weight * (shifted(padded, 3, length, axis) - shifted(padded, 0, length, axis))

def forward_diff(padded, length, axis):
    return near_weight * (shifted(padded, 3, length, axis) - shifted(padded, 2, length, axis)) + far_weight * (shifted(padded, 4, length, axis) - shifted(padded, 1, length, axis))

def padded_three(field):
    return (jnp.pad(field, ((0, 0), (2, 2), (0, 0), (0, 0))), jnp.pad(field, ((0, 0), (0, 0), (2, 2), (0, 0))), jnp.pad(field, ((0, 0), (0, 0), (0, 0), (2, 2))))

def advance(velocity, stress, lame_first, shear_modulus, buoyancy, strain_now, surface, lame_kernel, shear_kernel):
    cells_first = velocity.shape[1]
    cells_second = velocity.shape[2]
    cells_third = velocity.shape[3]
    stress_first, stress_second, stress_third = padded_three(stress)
    force_first = forward_diff(stress_first[0], cells_first, 0) + backward_diff(stress_second[3], cells_second, 1) + backward_diff(stress_third[4], cells_third, 2)
    force_second = backward_diff(stress_first[3], cells_first, 0) + forward_diff(stress_second[1], cells_second, 1) + backward_diff(stress_third[5], cells_third, 2)
    force_third = backward_diff(stress_first[4], cells_first, 0) + backward_diff(stress_second[5], cells_second, 1) + forward_diff(stress_third[2], cells_third, 2)
    force_third = force_third.at[:, :, 0].add(surface)
    moved = velocity + time_step * buoyancy[None] * jnp.stack([force_first, force_second, force_third])
    motion_first, motion_second, motion_third = padded_three(moved)
    rate_first = backward_diff(motion_first[0], cells_first, 0)
    rate_second = backward_diff(motion_second[1], cells_second, 1)
    rate_third = backward_diff(motion_third[2], cells_third, 2)
    shear_one = forward_diff(motion_second[0], cells_second, 1) + forward_diff(motion_first[1], cells_first, 0)
    shear_two = forward_diff(motion_third[0], cells_third, 2) + forward_diff(motion_first[2], cells_first, 0)
    shear_three = forward_diff(motion_third[1], cells_third, 2) + forward_diff(motion_second[2], cells_second, 1)
    dilation = rate_first + rate_second + rate_third
    grown = stress + time_step * jnp.stack([lame_first * dilation + 2.0 * shear_modulus * rate_first, lame_first * dilation + 2.0 * shear_modulus * rate_second, lame_first * dilation + 2.0 * shear_modulus * rate_third, shear_modulus * shear_one, shear_modulus * shear_two, shear_modulus * shear_three])
    strain_vals = strain_now.astype(jnp.float32)
    lame_kernel = lame_kernel + time_step * (strain_vals[0] + strain_vals[1] + strain_vals[2]) * dilation
    shear_kernel = shear_kernel + 2.0 * time_step * (strain_vals[0] * rate_first + strain_vals[1] * rate_second + strain_vals[2] * rate_third + strain_vals[3] * shear_one + strain_vals[4] * shear_two + strain_vals[5] * shear_three)
    return (moved, grown, lame_kernel, shear_kernel)

def reference(velocity, stress, lame_first, shear_modulus, buoyancy, forward_strain, lame_accum, shear_accum, residuals, station_cell, station_pairs):
    values = residuals.astype(jnp.float32)
    normed = values / jnp.sqrt(lax.optimization_barrier(jnp.mean(values * values, axis=1, keepdims=True)) + epsilon)
    blocks = station_pairs.reshape(PAIRS // P_DEV, P_DEV, 2)

    def add_block(total, block):
        first_vals = normed[block[:, 0]]
        second_vals = normed[block[:, 1]]
        corr = lax.optimization_barrier(jnp.mean(first_vals * second_vals, axis=1, keepdims=True))
        toward_first = lax.optimization_barrier((second_vals - corr * first_vals).astype(jnp.bfloat16)).astype(jnp.float32)
        toward_second = lax.optimization_barrier((first_vals - corr * second_vals).astype(jnp.bfloat16)).astype(jnp.float32)
        total = total.at[block[:, 0]].add(toward_first)
        total = total.at[block[:, 1]].add(toward_second)
        return (total, None)
    adjoint, ignored = lax.scan(add_block, jnp.zeros((STATIONS, NSAMP), jnp.float32), blocks)
    holder = (jnp.arange(STATIONS) // STA_DEV).astype(jnp.int32)
    across_pos = (holder // N_GY * CX + station_cell // CY).astype(jnp.int32)
    along_pos = (holder % N_GY * CY + station_cell % CY).astype(jnp.int32)
    for window_step in range(STEPS):
        surface = jnp.zeros((NX, NY), jnp.float32).at[across_pos, along_pos].add(adjoint[:, NSAMP - 1 - window_step])
        strain_now = forward_strain[6 * window_step:6 * window_step + 6]
        velocity, stress, lame_accum, shear_accum = advance(velocity, stress, lame_first, shear_modulus, buoyancy, strain_now, surface, lame_accum, shear_accum)
    return (velocity, stress, lame_accum, shear_accum, adjoint)
```

```python
import jax
import jax.numpy as jnp
from jax import lax
from jax.sharding import PartitionSpec as P

near_weight = 9.0 / 8.0
far_weight = -1.0 / 24.0
time_step = 0.25
epsilon = 1e-06


def shifted(padded, start, length, axis):
    return lax.slice_in_dim(padded, start, start + length, axis=axis)


def backward_diff(padded, length, axis):
    return near_weight * (
        shifted(padded, 2, length, axis) - shifted(padded, 1, length, axis)
    ) + far_weight * (shifted(padded, 3, length, axis) - shifted(padded, 0, length, axis))


def forward_diff(padded, length, axis):
    return near_weight * (
        shifted(padded, 3, length, axis) - shifted(padded, 2, length, axis)
    ) + far_weight * (shifted(padded, 4, length, axis) - shifted(padded, 1, length, axis))


def halo_pad(block, axis, dim, width=2):
    count = lax.axis_size(axis)
    forward = [(i, i + 1) for i in range(count - 1)]
    backward = [(i + 1, i) for i in range(count - 1)]
    size = block.shape[dim]
    low = lax.ppermute(lax.slice_in_dim(block, size - width, size, axis=dim), axis, forward)
    high = lax.ppermute(lax.slice_in_dim(block, 0, width, axis=dim), axis, backward)
    return jnp.concatenate([low, block, high], axis=dim)


def z_pad(block):
    pads = [(0, 0)] * (block.ndim - 1) + [(2, 2)]
    return jnp.pad(block, pads)


def advance(velocity, stress, lame_first, shear_modulus, buoyancy, strain_now, surface, lame_kernel, shear_kernel):
    nx = velocity.shape[1]
    ny = velocity.shape[2]
    nz = velocity.shape[3]
    sx = halo_pad(jnp.stack([stress[0], stress[3], stress[4]]), "gx", 1)
    sy = halo_pad(jnp.stack([stress[3], stress[1], stress[5]]), "gy", 2)
    sz = z_pad(jnp.stack([stress[4], stress[5], stress[2]]))
    force_first = forward_diff(sx[0], nx, 0) + backward_diff(sy[0], ny, 1) + backward_diff(sz[0], nz, 2)
    force_second = backward_diff(sx[1], nx, 0) + forward_diff(sy[1], ny, 1) + backward_diff(sz[1], nz, 2)
    force_third = backward_diff(sx[2], nx, 0) + backward_diff(sy[2], ny, 1) + forward_diff(sz[2], nz, 2)
    force_third = force_third.at[:, :, 0].add(surface)
    moved = velocity + time_step * buoyancy[None] * jnp.stack([force_first, force_second, force_third])
    mx = halo_pad(moved, "gx", 1)
    my = halo_pad(moved, "gy", 2)
    mz = z_pad(moved)
    rate_first = backward_diff(mx[0], nx, 0)
    rate_second = backward_diff(my[1], ny, 1)
    rate_third = backward_diff(mz[2], nz, 2)
    shear_one = forward_diff(my[0], ny, 1) + forward_diff(mx[1], nx, 0)
    shear_two = forward_diff(mz[0], nz, 2) + forward_diff(mx[2], nx, 0)
    shear_three = forward_diff(mz[1], nz, 2) + forward_diff(my[2], ny, 1)
    dilation = rate_first + rate_second + rate_third
    grown = stress + time_step * jnp.stack(
        [
            lame_first * dilation + 2.0 * shear_modulus * rate_first,
            lame_first * dilation + 2.0 * shear_modulus * rate_second,
            lame_first * dilation + 2.0 * shear_modulus * rate_third,
            shear_modulus * shear_one,
            shear_modulus * shear_two,
            shear_modulus * shear_three,
        ]
    )
    strain_vals = strain_now.astype(jnp.float32)
    lame_kernel = lame_kernel + time_step * (strain_vals[0] + strain_vals[1] + strain_vals[2]) * dilation
    shear_kernel = shear_kernel + 2.0 * time_step * (
        strain_vals[0] * rate_first
        + strain_vals[1] * rate_second
        + strain_vals[2] * rate_third
        + strain_vals[3] * shear_one
        + strain_vals[4] * shear_two
        + strain_vals[5] * shear_three
    )
    return (moved, grown, lame_kernel, shear_kernel)


def station_part(residuals, station_cell, station_pairs, cells_first, cells_second, step_count):
    stations_here = residuals.shape[0]
    samples = residuals.shape[1]
    devices = lax.axis_size(("gx", "gy"))
    pair_rows = station_pairs.shape[0] // devices
    me = lax.axis_index(("gx", "gy"))
    own = lax.dynamic_slice_in_dim(station_pairs, me * pair_rows, pair_rows, 0)
    first_local = own[:, 0] - me * stations_here
    dest = own[:, 1] // stations_here
    order = jnp.arange(pair_rows)
    same = (dest[:, None] == dest[None, :]) & (order[None, :] < order[:, None])
    rank = jnp.sum(same.astype(jnp.int32), axis=1)
    device_ids = jnp.arange(devices)
    pick_own = (dest[None, :, None] == device_ids[:, None, None]) & (rank[None, :, None] == jnp.arange(2)[None, None, :])
    own_station = jnp.sum(jnp.where(pick_own, first_local[None, :, None] + 1, 0), axis=1) - 1
    blocks = station_pairs.reshape(devices, pair_rows, 2)
    hit = (blocks[:, :, 1] // stations_here == me).astype(jnp.int32)
    before = jnp.cumsum(hit, axis=1) - hit
    pick_in = (hit[:, :, None] > 0) & (before[:, :, None] == jnp.arange(2)[None, None, :])
    in_station = jnp.sum(jnp.where(pick_in, (blocks[:, :, 1] % stations_here)[:, :, None] + 1, 0), axis=1) - 1
    slot_station = jnp.concatenate([own_station, in_station], axis=1)
    hits = (slot_station[:, :, None] == jnp.arange(stations_here)[None, None, :]).astype(jnp.bfloat16)
    lanes = 128
    rows = residuals.reshape(stations_here, samples // lanes, lanes)
    send = jnp.einsum("xjs,sab->xjab", hits, rows)
    recv = lax.all_to_all(send, ("gx", "gy"), split_axis=0, concat_axis=0, tiled=True)
    partner = jnp.concatenate([recv[:, 2:4], recv[:, 0:2]], axis=1)
    mine_vals = send.astype(jnp.float32)
    other_vals = partner.astype(jnp.float32)
    mine_norm = jnp.sqrt(jnp.mean(mine_vals * mine_vals, axis=(2, 3), keepdims=True) + epsilon)
    other_norm = jnp.sqrt(jnp.mean(other_vals * other_vals, axis=(2, 3), keepdims=True) + epsilon)
    corr = jnp.mean(mine_vals * other_vals, axis=(2, 3), keepdims=True) / (mine_norm * other_norm)
    toward = (other_vals / other_norm - corr * (mine_vals / mine_norm)).astype(jnp.bfloat16)
    adjoint3 = jnp.einsum("xjs,xjab->sab", hits, toward, preferred_element_type=jnp.float32)
    adjoint = adjoint3.reshape(stations_here, samples)
    tail = jnp.einsum(
        "xjs,xjk->sk", hits, toward[:, :, -1, lanes - step_count :], preferred_element_type=jnp.float32
    )
    cells_hit = (station_cell[:, None] == jnp.arange(cells_first * cells_second)[None, :]).astype(jnp.float32)
    surfaces = jnp.stack(
        [
            jnp.sum(cells_hit * tail[:, step_count - 1 - window_step][:, None], axis=0).reshape(cells_first, cells_second)
            for window_step in range(step_count)
        ]
    )
    return adjoint, surfaces


def shards(velocity, stress, lame_first, shear_modulus, buoyancy, forward_strain, lame_accum, shear_accum, residuals, station_cell, station_pairs):
    step_count = forward_strain.shape[0] // 6
    adjoint, surfaces = station_part(residuals, station_cell, station_pairs, velocity.shape[1], velocity.shape[2], step_count)
    for window_step in range(step_count):
        strain_now = forward_strain[6 * window_step : 6 * window_step + 6]
        velocity, stress, lame_accum, shear_accum = advance(
            velocity, stress, lame_first, shear_modulus, buoyancy, strain_now, surfaces[window_step], lame_accum, shear_accum
        )
    return (velocity, stress, lame_accum, shear_accum, adjoint)


def solution(mesh):
    return jax.shard_map(
        shards,
        mesh=mesh,
        in_specs=(
            P(None, "gx", "gy", None),
            P(None, "gx", "gy", None),
            P("gx", "gy", None),
            P("gx", "gy", None),
            P("gx", "gy", None),
            P(None, "gx", "gy", None),
            P("gx", "gy", None),
            P("gx", "gy", None),
            P(("gx", "gy"), None),
            P(("gx", "gy")),
            P(),
        ),
        out_specs=(
            P(None, "gx", "gy", None),
            P(None, "gx", "gy", None),
            P("gx", "gy", None),
            P("gx", "gy", None),
            P(("gx", "gy"), None),
        ),
        check_vma=False,
    )
```

```python
import jax
import jax.numpy as jnp
from jax import lax
from jax.sharding import PartitionSpec as P

near_weight = 9.0 / 8.0
far_weight = -1.0 / 24.0
time_step = 0.25
epsilon = 1e-06


def shifted(padded, start, length, axis):
    return lax.slice_in_dim(padded, start, start + length, axis=axis)


def backward_diff(padded, length, axis):
    return near_weight * (
        shifted(padded, 2, length, axis) - shifted(padded, 1, length, axis)
    ) + far_weight * (shifted(padded, 3, length, axis) - shifted(padded, 0, length, axis))


def forward_diff(padded, length, axis):
    return near_weight * (
        shifted(padded, 3, length, axis) - shifted(padded, 2, length, axis)
    ) + far_weight * (shifted(padded, 4, length, axis) - shifted(padded, 1, length, axis))


def halo_pad(block, axis, dim, width=2):
    count = lax.axis_size(axis)
    forward = [(i, i + 1) for i in range(count - 1)]
    backward = [(i + 1, i) for i in range(count - 1)]
    size = block.shape[dim]
    low = lax.ppermute(lax.slice_in_dim(block, size - width, size, axis=dim), axis, forward)
    high = lax.ppermute(lax.slice_in_dim(block, 0, width, axis=dim), axis, backward)
    return jnp.concatenate([low, block, high], axis=dim)


def z_pad(block):
    pads = [(0, 0)] * (block.ndim - 1) + [(2, 2)]
    return jnp.pad(block, pads)


def advance(velocity, stress, lame_first, shear_modulus, buoyancy, strain_now, surface, lame_kernel, shear_kernel):
    nx = velocity.shape[1]
    ny = velocity.shape[2]
    nz = velocity.shape[3]
    sx = halo_pad(jnp.stack([stress[0], stress[3], stress[4]]), "gx", 1)
    sy = halo_pad(jnp.stack([stress[3], stress[1], stress[5]]), "gy", 2)
    sz = z_pad(jnp.stack([stress[4], stress[5], stress[2]]))
    force_first = forward_diff(sx[0], nx, 0) + backward_diff(sy[0], ny, 1) + backward_diff(sz[0], nz, 2)
    force_second = backward_diff(sx[1], nx, 0) + forward_diff(sy[1], ny, 1) + backward_diff(sz[1], nz, 2)
    force_third = backward_diff(sx[2], nx, 0) + backward_diff(sy[2], ny, 1) + forward_diff(sz[2], nz, 2)
    force_third = force_third.at[:, :, 0].add(surface)
    moved = velocity + time_step * buoyancy[None] * jnp.stack([force_first, force_second, force_third])
    mx = halo_pad(moved, "gx", 1)
    my = halo_pad(moved, "gy", 2)
    mz = z_pad(moved)
    rate_first = backward_diff(mx[0], nx, 0)
    rate_second = backward_diff(my[1], ny, 1)
    rate_third = backward_diff(mz[2], nz, 2)
    shear_one = forward_diff(my[0], ny, 1) + forward_diff(mx[1], nx, 0)
    shear_two = forward_diff(mz[0], nz, 2) + forward_diff(mx[2], nx, 0)
    shear_three = forward_diff(mz[1], nz, 2) + forward_diff(my[2], ny, 1)
    dilation = rate_first + rate_second + rate_third
    grown = stress + time_step * jnp.stack(
        [
            lame_first * dilation + 2.0 * shear_modulus * rate_first,
            lame_first * dilation + 2.0 * shear_modulus * rate_second,
            lame_first * dilation + 2.0 * shear_modulus * rate_third,
            shear_modulus * shear_one,
            shear_modulus * shear_two,
            shear_modulus * shear_three,
        ]
    )
    strain_vals = strain_now.astype(jnp.float32)
    lame_kernel = lame_kernel + time_step * (strain_vals[0] + strain_vals[1] + strain_vals[2]) * dilation
    shear_kernel = shear_kernel + 2.0 * time_step * (
        strain_vals[0] * rate_first
        + strain_vals[1] * rate_second
        + strain_vals[2] * rate_third
        + strain_vals[3] * shear_one
        + strain_vals[4] * shear_two
        + strain_vals[5] * shear_three
    )
    return (moved, grown, lame_kernel, shear_kernel)


def station_part(residuals, station_cell, station_pairs, cells_first, cells_second, step_count):
    stations_here = residuals.shape[0]
    samples = residuals.shape[1]
    devices = lax.axis_size(("gx", "gy"))
    pair_rows = station_pairs.shape[0] // devices
    me = lax.axis_index(("gx", "gy"))
    own = lax.dynamic_slice_in_dim(station_pairs, me * pair_rows, pair_rows, 0)
    first_local = own[:, 0] - me * stations_here
    dest = own[:, 1] // stations_here
    order = jnp.arange(pair_rows)
    same = (dest[:, None] == dest[None, :]) & (order[None, :] < order[:, None])
    rank = jnp.sum(same.astype(jnp.int32), axis=1)
    device_ids = jnp.arange(devices)
    pick_own = (dest[None, :, None] == device_ids[:, None, None]) & (rank[None, :, None] == jnp.arange(2)[None, None, :])
    own_station = jnp.sum(jnp.where(pick_own, first_local[None, :, None] + 1, 0), axis=1) - 1
    blocks = station_pairs.reshape(devices, pair_rows, 2)
    hit = (blocks[:, :, 1] // stations_here == me).astype(jnp.int32)
    before = jnp.cumsum(hit, axis=1) - hit
    pick_in = (hit[:, :, None] > 0) & (before[:, :, None] == jnp.arange(2)[None, None, :])
    in_station = jnp.sum(jnp.where(pick_in, (blocks[:, :, 1] % stations_here)[:, :, None] + 1, 0), axis=1) - 1
    slot_station = jnp.concatenate([own_station, in_station], axis=1)
    lanes = 128
    rows = residuals.reshape(stations_here, samples // lanes, lanes)
    send = jnp.where(
        (slot_station >= 0)[:, :, None, None], rows[jnp.maximum(slot_station, 0)], jnp.zeros((), residuals.dtype)
    )
    recv = lax.all_to_all(send, ("gx", "gy"), split_axis=0, concat_axis=0, tiled=True)
    mine_station = jnp.concatenate([slot_station[:, 2:4], slot_station[:, 0:2]], axis=1)
    mine = jnp.where(
        (mine_station >= 0)[:, :, None, None], rows[jnp.maximum(mine_station, 0)], jnp.zeros((), residuals.dtype)
    )
    mine_vals = mine.astype(jnp.float32)
    other_vals = recv.astype(jnp.float32)
    mine_norm = jnp.sqrt(jnp.mean(mine_vals * mine_vals, axis=(2, 3), keepdims=True) + epsilon)
    other_norm = jnp.sqrt(jnp.mean(other_vals * other_vals, axis=(2, 3), keepdims=True) + epsilon)
    corr = jnp.mean(mine_vals * other_vals, axis=(2, 3), keepdims=True) / (mine_norm * other_norm)
    toward = (other_vals / other_norm - corr * (mine_vals / mine_norm)).astype(jnp.bfloat16)
    slots = devices * 4
    hits = (mine_station.reshape(slots)[:, None] == jnp.arange(stations_here)[None, :]).astype(jnp.bfloat16)
    flat = toward.reshape(slots, samples)
    adjoint = lax.dot_general(hits, flat, (((0,), (0,)), ((), ())), preferred_element_type=jnp.float32)
    tail = lax.dot_general(
        hits, flat[:, samples - step_count :], (((0,), (0,)), ((), ())), preferred_element_type=jnp.float32
    )
    cells_hit = (station_cell[:, None] == jnp.arange(cells_first * cells_second)[None, :]).astype(jnp.float32)
    surfaces = jnp.stack(
        [
            jnp.sum(cells_hit * tail[:, step_count - 1 - window_step][:, None], axis=0).reshape(cells_first, cells_second)
            for window_step in range(step_count)
        ]
    )
    return adjoint, surfaces


def shards(velocity, stress, lame_first, shear_modulus, buoyancy, forward_strain, lame_accum, shear_accum, residuals, station_cell, station_pairs):
    step_count = forward_strain.shape[0] // 6
    adjoint, surfaces = station_part(residuals, station_cell, station_pairs, velocity.shape[1], velocity.shape[2], step_count)
    for window_step in range(step_count):
        strain_now = forward_strain[6 * window_step : 6 * window_step + 6]
        velocity, stress, lame_accum, shear_accum = advance(
            velocity, stress, lame_first, shear_modulus, buoyancy, strain_now, surfaces[window_step], lame_accum, shear_accum
        )
    return (velocity, stress, lame_accum, shear_accum, adjoint)


def solution(mesh):
    return jax.shard_map(
        shards,
        mesh=mesh,
        in_specs=(
            P(None, "gx", "gy", None),
            P(None, "gx", "gy", None),
            P("gx", "gy", None),
            P("gx", "gy", None),
            P("gx", "gy", None),
            P(None, "gx", "gy", None),
            P("gx", "gy", None),
            P("gx", "gy", None),
            P(("gx", "gy"), None),
            P(("gx", "gy")),
            P(),
        ),
        out_specs=(
            P(None, "gx", "gy", None),
            P(None, "gx", "gy", None),
            P("gx", "gy", None),
            P("gx", "gy", None),
            P(("gx", "gy"), None),
        ),
        check_vma=False,
    )
```

```python
import jax
import jax.numpy as jnp
from jax import lax
from jax.sharding import PartitionSpec as P

near_weight = 9.0 / 8.0
far_weight = -1.0 / 24.0
time_step = 0.25
epsilon = 1e-06


def shifted(padded, start, length, axis):
    return lax.slice_in_dim(padded, start, start + length, axis=axis)


def backward_diff(padded, length, axis):
    return near_weight * (
        shifted(padded, 2, length, axis) - shifted(padded, 1, length, axis)
    ) + far_weight * (shifted(padded, 3, length, axis) - shifted(padded, 0, length, axis))


def forward_diff(padded, length, axis):
    return near_weight * (
        shifted(padded, 3, length, axis) - shifted(padded, 2, length, axis)
    ) + far_weight * (shifted(padded, 4, length, axis) - shifted(padded, 1, length, axis))


def halo_pad(block, axis, dim, width=2):
    count = lax.axis_size(axis)
    forward = [(i, i + 1) for i in range(count - 1)]
    backward = [(i + 1, i) for i in range(count - 1)]
    size = block.shape[dim]
    low = lax.ppermute(lax.slice_in_dim(block, size - width, size, axis=dim), axis, forward)
    high = lax.ppermute(lax.slice_in_dim(block, 0, width, axis=dim), axis, backward)
    return jnp.concatenate([low, block, high], axis=dim)


def z_pad(block):
    pads = [(0, 0)] * (block.ndim - 1) + [(2, 2)]
    return jnp.pad(block, pads)


def halo_x(block):
    return halo_pad(block, "gx", 1)


def halo_y(block):
    return halo_pad(block, "gy", 2)


def zero_x(block):
    return jnp.pad(block, ((0, 0), (2, 2), (0, 0), (0, 0)))


def zero_y(block):
    return jnp.pad(block, ((0, 0), (0, 0), (2, 2), (0, 0)))


def advance(velocity, stress, lame_first, shear_modulus, buoyancy, strain_now, surface, lame_kernel, shear_kernel, pad_x, pad_y):
    nx = velocity.shape[1]
    ny = velocity.shape[2]
    nz = velocity.shape[3]
    sx = pad_x(jnp.stack([stress[0], stress[3], stress[4]]))
    sy = pad_y(jnp.stack([stress[3], stress[1], stress[5]]))
    sz = z_pad(jnp.stack([stress[4], stress[5], stress[2]]))
    force_first = forward_diff(sx[0], nx, 0) + backward_diff(sy[0], ny, 1) + backward_diff(sz[0], nz, 2)
    force_second = backward_diff(sx[1], nx, 0) + forward_diff(sy[1], ny, 1) + backward_diff(sz[1], nz, 2)
    force_third = backward_diff(sx[2], nx, 0) + backward_diff(sy[2], ny, 1) + forward_diff(sz[2], nz, 2)
    if surface is not None:
        force_third = force_third.at[:, :, 0].add(surface)
    moved = velocity + time_step * buoyancy[None] * jnp.stack([force_first, force_second, force_third])
    mx = pad_x(moved)
    my = pad_y(moved)
    mz = z_pad(moved)
    rate_first = backward_diff(mx[0], nx, 0)
    rate_second = backward_diff(my[1], ny, 1)
    rate_third = backward_diff(mz[2], nz, 2)
    shear_one = forward_diff(my[0], ny, 1) + forward_diff(mx[1], nx, 0)
    shear_two = forward_diff(mz[0], nz, 2) + forward_diff(mx[2], nx, 0)
    shear_three = forward_diff(mz[1], nz, 2) + forward_diff(my[2], ny, 1)
    dilation = rate_first + rate_second + rate_third
    grown = stress + time_step * jnp.stack(
        [
            lame_first * dilation + 2.0 * shear_modulus * rate_first,
            lame_first * dilation + 2.0 * shear_modulus * rate_second,
            lame_first * dilation + 2.0 * shear_modulus * rate_third,
            shear_modulus * shear_one,
            shear_modulus * shear_two,
            shear_modulus * shear_three,
        ]
    )
    strain_vals = strain_now.astype(jnp.float32)
    lame_kernel = lame_kernel + time_step * (strain_vals[0] + strain_vals[1] + strain_vals[2]) * dilation
    shear_kernel = shear_kernel + 2.0 * time_step * (
        strain_vals[0] * rate_first
        + strain_vals[1] * rate_second
        + strain_vals[2] * rate_third
        + strain_vals[3] * shear_one
        + strain_vals[4] * shear_two
        + strain_vals[5] * shear_three
    )
    return (moved, grown, lame_kernel, shear_kernel)


def station_part(residuals, station_cell, station_pairs, cells_first, cells_second, step_count):
    stations_here = residuals.shape[0]
    samples = residuals.shape[1]
    devices = lax.axis_size(("gx", "gy"))
    pair_rows = station_pairs.shape[0] // devices
    me = lax.axis_index(("gx", "gy"))
    own = lax.dynamic_slice_in_dim(station_pairs, me * pair_rows, pair_rows, 0)
    first_local = own[:, 0] - me * stations_here
    dest = own[:, 1] // stations_here
    order = jnp.arange(pair_rows)
    same = (dest[:, None] == dest[None, :]) & (order[None, :] < order[:, None])
    rank = jnp.sum(same.astype(jnp.int32), axis=1)
    device_ids = jnp.arange(devices)
    pick_own = (dest[None, :, None] == device_ids[:, None, None]) & (rank[None, :, None] == jnp.arange(2)[None, None, :])
    own_station = jnp.sum(jnp.where(pick_own, first_local[None, :, None] + 1, 0), axis=1) - 1
    blocks = station_pairs.reshape(devices, pair_rows, 2)
    hit = (blocks[:, :, 1] // stations_here == me).astype(jnp.int32)
    before = jnp.cumsum(hit, axis=1) - hit
    pick_in = (hit[:, :, None] > 0) & (before[:, :, None] == jnp.arange(2)[None, None, :])
    in_station = jnp.sum(jnp.where(pick_in, (blocks[:, :, 1] % stations_here)[:, :, None] + 1, 0), axis=1) - 1
    slot_station = jnp.concatenate([own_station, in_station], axis=1)
    lanes = 128
    rows = residuals.reshape(stations_here, samples // lanes, lanes)
    send = jnp.where(
        (slot_station >= 0)[:, :, None, None], rows[jnp.maximum(slot_station, 0)], jnp.zeros((), residuals.dtype)
    )
    recv = lax.all_to_all(send, ("gx", "gy"), split_axis=0, concat_axis=0, tiled=True)
    mine_station = jnp.concatenate([slot_station[:, 2:4], slot_station[:, 0:2]], axis=1)
    mine = jnp.where(
        (mine_station >= 0)[:, :, None, None], rows[jnp.maximum(mine_station, 0)], jnp.zeros((), residuals.dtype)
    )
    mine_vals = mine.astype(jnp.float32)
    other_vals = recv.astype(jnp.float32)
    mine_norm = jnp.sqrt(jnp.mean(mine_vals * mine_vals, axis=(2, 3), keepdims=True) + epsilon)
    other_norm = jnp.sqrt(jnp.mean(other_vals * other_vals, axis=(2, 3), keepdims=True) + epsilon)
    corr = jnp.mean(mine_vals * other_vals, axis=(2, 3), keepdims=True) / (mine_norm * other_norm)
    toward = (other_vals / other_norm - corr * (mine_vals / mine_norm)).astype(jnp.bfloat16)
    slots = devices * 4
    hits = (mine_station.reshape(slots)[:, None] == jnp.arange(stations_here)[None, :]).astype(jnp.bfloat16)
    flat = toward.reshape(slots, samples)
    adjoint = lax.dot_general(hits, flat, (((0,), (0,)), ((), ())), preferred_element_type=jnp.float32)
    tail = lax.dot_general(
        hits, flat[:, samples - step_count :], (((0,), (0,)), ((), ())), preferred_element_type=jnp.float32
    )
    cells_hit = (station_cell[:, None] == jnp.arange(cells_first * cells_second)[None, :]).astype(jnp.float32)
    surfaces = jnp.stack(
        [
            jnp.sum(cells_hit * tail[:, step_count - 1 - window_step][:, None], axis=0).reshape(cells_first, cells_second)
            for window_step in range(step_count)
        ]
    )
    return adjoint, surfaces


def wide_halo(block, width):
    return halo_pad(halo_pad(block, "gx", 1, width), "gy", 2, width)


def shards(velocity, stress, lame_first, shear_modulus, buoyancy, forward_strain, lame_accum, shear_accum, residuals, station_cell, station_pairs):
    step_count = forward_strain.shape[0] // 6
    nx = velocity.shape[1]
    ny = velocity.shape[2]
    reach = 6
    depth = 8
    adjoint, surfaces = station_part(residuals, station_cell, station_pairs, nx, ny, step_count)
    free_v, free_s, free_l, free_k = velocity, stress, lame_accum, shear_accum
    for window_step in range(step_count):
        strain_now = forward_strain[6 * window_step : 6 * window_step + 6]
        free_v, free_s, free_l, free_k = advance(
            free_v, free_s, lame_first, shear_modulus, buoyancy, strain_now, None, free_l, free_k, halo_x, halo_y
        )
    params = wide_halo(jnp.stack([lame_first, shear_modulus, buoyancy])[:, :, :, :depth], reach)
    gathered = lax.all_gather(surfaces, ("gx", "gy"), tiled=False)
    rows_x = lax.axis_size("gx")
    rows_y = lax.axis_size("gy")
    whole = gathered.reshape(rows_x, rows_y, step_count, nx, ny).transpose(2, 0, 3, 1, 4)
    whole = whole.reshape(step_count, rows_x * nx, rows_y * ny)
    whole = jnp.pad(whole, ((0, 0), (reach, reach), (reach, reach)))
    near = lax.dynamic_slice(
        whole, (0, lax.axis_index("gx") * nx, lax.axis_index("gy") * ny), (step_count, nx + 2 * reach, ny + 2 * reach)
    )
    wx = nx + 2 * reach
    wy = ny + 2 * reach
    src_v = jnp.zeros((3, wx, wy, depth), jnp.float32)
    src_s = jnp.zeros((6, wx, wy, depth), jnp.float32)
    src_l = jnp.zeros((wx, wy, depth), jnp.float32)
    src_k = jnp.zeros((wx, wy, depth), jnp.float32)
    for window_step in range(step_count):
        strain_now = forward_strain[6 * window_step : 6 * window_step + 6, :, :, :depth]
        strain_now = jnp.pad(strain_now, ((0, 0), (reach, reach), (reach, reach), (0, 0)))
        src_v, src_s, src_l, src_k = advance(
            src_v, src_s, params[0], params[1], params[2], strain_now, near[window_step], src_l, src_k, zero_x, zero_y
        )
    inner = (slice(reach, reach + nx), slice(reach, reach + ny))
    velocity = free_v.at[:, :, :, :depth].add(src_v[(slice(None),) + inner])
    stress = free_s.at[:, :, :, :depth].add(src_s[(slice(None),) + inner])
    lame_accum = free_l.at[:, :, :depth].add(src_l[inner])
    shear_accum = free_k.at[:, :, :depth].add(src_k[inner])
    return (velocity, stress, lame_accum, shear_accum, adjoint)


def solution(mesh):
    return jax.shard_map(
        shards,
        mesh=mesh,
        in_specs=(
            P(None, "gx", "gy", None),
            P(None, "gx", "gy", None),
            P("gx", "gy", None),
            P("gx", "gy", None),
            P("gx", "gy", None),
            P(None, "gx", "gy", None),
            P("gx", "gy", None),
            P("gx", "gy", None),
            P(("gx", "gy"), None),
            P(("gx", "gy")),
            P(),
        ),
        out_specs=(
            P(None, "gx", "gy", None),
            P(None, "gx", "gy", None),
            P("gx", "gy", None),
            P("gx", "gy", None),
            P(("gx", "gy"), None),
        ),
        check_vma=False,
    )
```

```python
import functools

import jax
import jax.numpy as jnp
from jax import lax
from jax.sharding import PartitionSpec as P
from jax.experimental import pallas as pl
from jax.experimental.pallas import tpu as pltpu

near_weight = 9.0 / 8.0
far_weight = -1.0 / 24.0
time_step = 0.25
epsilon = 1e-06


def shifted(padded, start, length, axis):
    return lax.slice_in_dim(padded, start, start + length, axis=axis)


def backward_diff(padded, length, axis):
    return near_weight * (
        shifted(padded, 2, length, axis) - shifted(padded, 1, length, axis)
    ) + far_weight * (shifted(padded, 3, length, axis) - shifted(padded, 0, length, axis))


def forward_diff(padded, length, axis):
    return near_weight * (
        shifted(padded, 3, length, axis) - shifted(padded, 2, length, axis)
    ) + far_weight * (shifted(padded, 4, length, axis) - shifted(padded, 1, length, axis))


def halo_pad(block, axis, dim, width=2):
    count = lax.axis_size(axis)
    forward = [(i, i + 1) for i in range(count - 1)]
    backward = [(i + 1, i) for i in range(count - 1)]
    size = block.shape[dim]
    low = lax.ppermute(lax.slice_in_dim(block, size - width, size, axis=dim), axis, forward)
    high = lax.ppermute(lax.slice_in_dim(block, 0, width, axis=dim), axis, backward)
    return jnp.concatenate([low, block, high], axis=dim)


def z_pad(block):
    pads = [(0, 0)] * (block.ndim - 1) + [(2, 2)]
    return jnp.pad(block, pads)


def advance(velocity, stress, lame_first, shear_modulus, buoyancy, strain_now, surface, lame_kernel, shear_kernel):
    nx = velocity.shape[1]
    ny = velocity.shape[2]
    nz = velocity.shape[3]
    sx = halo_pad(jnp.stack([stress[0], stress[3], stress[4]]), "gx", 1)
    sy = halo_pad(jnp.stack([stress[3], stress[1], stress[5]]), "gy", 2)
    sz = z_pad(jnp.stack([stress[4], stress[5], stress[2]]))
    force_first = forward_diff(sx[0], nx, 0) + backward_diff(sy[0], ny, 1) + backward_diff(sz[0], nz, 2)
    force_second = backward_diff(sx[1], nx, 0) + forward_diff(sy[1], ny, 1) + backward_diff(sz[1], nz, 2)
    force_third = backward_diff(sx[2], nx, 0) + backward_diff(sy[2], ny, 1) + forward_diff(sz[2], nz, 2)
    force_third = force_third.at[:, :, 0].add(surface)
    moved = velocity + time_step * buoyancy[None] * jnp.stack([force_first, force_second, force_third])
    mx = halo_pad(moved, "gx", 1)
    my = halo_pad(moved, "gy", 2)
    mz = z_pad(moved)
    rate_first = backward_diff(mx[0], nx, 0)
    rate_second = backward_diff(my[1], ny, 1)
    rate_third = backward_diff(mz[2], nz, 2)
    shear_one = forward_diff(my[0], ny, 1) + forward_diff(mx[1], nx, 0)
    shear_two = forward_diff(mz[0], nz, 2) + forward_diff(mx[2], nx, 0)
    shear_three = forward_diff(mz[1], nz, 2) + forward_diff(my[2], ny, 1)
    dilation = rate_first + rate_second + rate_third
    grown = stress + time_step * jnp.stack(
        [
            lame_first * dilation + 2.0 * shear_modulus * rate_first,
            lame_first * dilation + 2.0 * shear_modulus * rate_second,
            lame_first * dilation + 2.0 * shear_modulus * rate_third,
            shear_modulus * shear_one,
            shear_modulus * shear_two,
            shear_modulus * shear_three,
        ]
    )
    strain_vals = strain_now.astype(jnp.float32)
    lame_kernel = lame_kernel + time_step * (strain_vals[0] + strain_vals[1] + strain_vals[2]) * dilation
    shear_kernel = shear_kernel + 2.0 * time_step * (
        strain_vals[0] * rate_first
        + strain_vals[1] * rate_second
        + strain_vals[2] * rate_third
        + strain_vals[3] * shear_one
        + strain_vals[4] * shear_two
        + strain_vals[5] * shear_three
    )
    return (moved, grown, lame_kernel, shear_kernel)


def pair_kernel(block, samples, station_ref, mine_ref, other_ref, out_ref, acc_ref, toward_ref):
    step = pl.program_id(0)

    @pl.when(step == 0)
    def _():
        acc_ref[...] = jnp.zeros_like(acc_ref)

    mine_vals = mine_ref[...].astype(jnp.float32)
    other_vals = other_ref[...].astype(jnp.float32)
    mine_sq = jnp.sum(jnp.sum(mine_vals * mine_vals, axis=2, keepdims=True), axis=1, keepdims=True)
    other_sq = jnp.sum(jnp.sum(other_vals * other_vals, axis=2, keepdims=True), axis=1, keepdims=True)
    cross = jnp.sum(jnp.sum(mine_vals * other_vals, axis=2, keepdims=True), axis=1, keepdims=True)
    mine_norm = jnp.sqrt(mine_sq / samples + epsilon)
    other_norm = jnp.sqrt(other_sq / samples + epsilon)
    corr = (cross / samples) / (mine_norm * other_norm)
    toward = other_vals / other_norm - corr * (mine_vals / mine_norm)
    toward_ref[...] = toward.astype(jnp.bfloat16).astype(jnp.float32)

    def add_one(i, carry):
        target = station_ref[step * block + i]
        acc_ref[target] = acc_ref[target] + toward_ref[i]
        return carry

    lax.fori_loop(0, block, add_one, 0)

    @pl.when(step == pl.num_programs(0) - 1)
    def _():
        out_ref[...] = acc_ref[: out_ref.shape[0]]


def pair_sums(targets, mine, other, stations):
    slots, rows, lanes = mine.shape
    block = 64
    samples = rows * lanes
    spec = pl.BlockSpec((block, rows, lanes), lambda g, t: (g, 0, 0))
    return pl.pallas_call(
        functools.partial(pair_kernel, block, float(samples)),
        grid_spec=pltpu.PrefetchScalarGridSpec(
            num_scalar_prefetch=1,
            grid=(slots // block,),
            in_specs=[spec, spec],
            out_specs=pl.BlockSpec((stations, rows, lanes), lambda g, t: (0, 0, 0)),
            scratch_shapes=[
                pltpu.VMEM((stations + 1, rows, lanes), jnp.float32),
                pltpu.VMEM((block, rows, lanes), jnp.float32),
            ],
        ),
        out_shape=jax.ShapeDtypeStruct((stations, rows, lanes), jnp.float32),
        compiler_params=pltpu.CompilerParams(dimension_semantics=("arbitrary",)),
        cost_estimate=pl.CostEstimate(flops=20 * slots * samples, transcendentals=0, bytes_accessed=4 * slots * samples),
    )(targets, mine, other)


def station_part(residuals, station_cell, station_pairs, cells_first, cells_second, step_count):
    stations_here = residuals.shape[0]
    samples = residuals.shape[1]
    devices = lax.axis_size(("gx", "gy"))
    pair_rows = station_pairs.shape[0] // devices
    me = lax.axis_index(("gx", "gy"))
    own = lax.dynamic_slice_in_dim(station_pairs, me * pair_rows, pair_rows, 0)
    first_local = own[:, 0] - me * stations_here
    dest = own[:, 1] // stations_here
    order = jnp.arange(pair_rows)
    same = (dest[:, None] == dest[None, :]) & (order[None, :] < order[:, None])
    rank = jnp.sum(same.astype(jnp.int32), axis=1)
    device_ids = jnp.arange(devices)
    pick_own = (dest[None, :, None] == device_ids[:, None, None]) & (rank[None, :, None] == jnp.arange(2)[None, None, :])
    own_station = jnp.sum(jnp.where(pick_own, first_local[None, :, None] + 1, 0), axis=1) - 1
    blocks = station_pairs.reshape(devices, pair_rows, 2)
    hit = (blocks[:, :, 1] // stations_here == me).astype(jnp.int32)
    before = jnp.cumsum(hit, axis=1) - hit
    pick_in = (hit[:, :, None] > 0) & (before[:, :, None] == jnp.arange(2)[None, None, :])
    in_station = jnp.sum(jnp.where(pick_in, (blocks[:, :, 1] % stations_here)[:, :, None] + 1, 0), axis=1) - 1
    slot_station = jnp.concatenate([own_station, in_station], axis=1)
    lanes = 128
    rows = residuals.reshape(stations_here, samples // lanes, lanes)
    send = jnp.where(
        (slot_station >= 0)[:, :, None, None], rows[jnp.maximum(slot_station, 0)], jnp.zeros((), residuals.dtype)
    )
    recv = lax.all_to_all(send, ("gx", "gy"), split_axis=0, concat_axis=0, tiled=True)
    mine_station = jnp.concatenate([slot_station[:, 2:4], slot_station[:, 0:2]], axis=1)
    mine = jnp.where(
        (mine_station >= 0)[:, :, None, None], rows[jnp.maximum(mine_station, 0)], jnp.zeros((), residuals.dtype)
    )
    slots = devices * 4
    targets = jnp.where(mine_station >= 0, mine_station, stations_here).reshape(slots)
    adjoint3 = pair_sums(
        targets, mine.reshape(slots, samples // lanes, lanes), recv.reshape(slots, samples // lanes, lanes), stations_here
    )
    adjoint = adjoint3.reshape(stations_here, samples)
    last = adjoint3[:, samples // lanes - 1, lanes - step_count :]
    tail = last
    cells_hit = (station_cell[:, None] == jnp.arange(cells_first * cells_second)[None, :]).astype(jnp.float32)
    surfaces = jnp.stack(
        [
            jnp.sum(cells_hit * tail[:, step_count - 1 - window_step][:, None], axis=0).reshape(cells_first, cells_second)
            for window_step in range(step_count)
        ]
    )
    return adjoint, surfaces


def shards(velocity, stress, lame_first, shear_modulus, buoyancy, forward_strain, lame_accum, shear_accum, residuals, station_cell, station_pairs):
    step_count = forward_strain.shape[0] // 6
    adjoint, surfaces = station_part(residuals, station_cell, station_pairs, velocity.shape[1], velocity.shape[2], step_count)
    for window_step in range(step_count):
        strain_now = forward_strain[6 * window_step : 6 * window_step + 6]
        velocity, stress, lame_accum, shear_accum = advance(
            velocity, stress, lame_first, shear_modulus, buoyancy, strain_now, surfaces[window_step], lame_accum, shear_accum
        )
    return (velocity, stress, lame_accum, shear_accum, adjoint)


def solution(mesh):
    return jax.shard_map(
        shards,
        mesh=mesh,
        in_specs=(
            P(None, "gx", "gy", None),
            P(None, "gx", "gy", None),
            P("gx", "gy", None),
            P("gx", "gy", None),
            P("gx", "gy", None),
            P(None, "gx", "gy", None),
            P("gx", "gy", None),
            P("gx", "gy", None),
            P(("gx", "gy"), None),
            P(("gx", "gy")),
            P(),
        ),
        out_specs=(
            P(None, "gx", "gy", None),
            P(None, "gx", "gy", None),
            P("gx", "gy", None),
            P("gx", "gy", None),
            P(("gx", "gy"), None),
        ),
        check_vma=False,
    )
```

```python
import functools

import jax
import jax.numpy as jnp
from jax import lax
from jax.sharding import PartitionSpec as P
from jax.experimental import pallas as pl
from jax.experimental.pallas import tpu as pltpu

near_weight = 9.0 / 8.0
far_weight = -1.0 / 24.0
time_step = 0.25
epsilon = 1e-06


def shifted(padded, start, length, axis):
    return lax.slice_in_dim(padded, start, start + length, axis=axis)


def backward_diff(padded, length, axis):
    return near_weight * (
        shifted(padded, 2, length, axis) - shifted(padded, 1, length, axis)
    ) + far_weight * (shifted(padded, 3, length, axis) - shifted(padded, 0, length, axis))


def forward_diff(padded, length, axis):
    return near_weight * (
        shifted(padded, 3, length, axis) - shifted(padded, 2, length, axis)
    ) + far_weight * (shifted(padded, 4, length, axis) - shifted(padded, 1, length, axis))


def halo_pad(block, axis, dim, width=2):
    count = lax.axis_size(axis)
    forward = [(i, i + 1) for i in range(count - 1)]
    backward = [(i + 1, i) for i in range(count - 1)]
    size = block.shape[dim]
    low = lax.ppermute(lax.slice_in_dim(block, size - width, size, axis=dim), axis, forward)
    high = lax.ppermute(lax.slice_in_dim(block, 0, width, axis=dim), axis, backward)
    return jnp.concatenate([low, block, high], axis=dim)


def z_pad(block):
    pads = [(0, 0)] * (block.ndim - 1) + [(2, 2)]
    return jnp.pad(block, pads)


def advance(velocity, stress, lame_first, shear_modulus, buoyancy, strain_now, surface, lame_kernel, shear_kernel):
    nx = velocity.shape[1]
    ny = velocity.shape[2]
    nz = velocity.shape[3]
    sx = halo_pad(jnp.stack([stress[0], stress[3], stress[4]]), "gx", 1)
    sy = halo_pad(jnp.stack([stress[3], stress[1], stress[5]]), "gy", 2)
    sz = z_pad(jnp.stack([stress[4], stress[5], stress[2]]))
    force_first = forward_diff(sx[0], nx, 0) + backward_diff(sy[0], ny, 1) + backward_diff(sz[0], nz, 2)
    force_second = backward_diff(sx[1], nx, 0) + forward_diff(sy[1], ny, 1) + backward_diff(sz[1], nz, 2)
    force_third = backward_diff(sx[2], nx, 0) + backward_diff(sy[2], ny, 1) + forward_diff(sz[2], nz, 2)
    force_third = force_third.at[:, :, 0].add(surface)
    moved = velocity + time_step * buoyancy[None] * jnp.stack([force_first, force_second, force_third])
    mx = halo_pad(moved, "gx", 1)
    my = halo_pad(moved, "gy", 2)
    mz = z_pad(moved)
    rate_first = backward_diff(mx[0], nx, 0)
    rate_second = backward_diff(my[1], ny, 1)
    rate_third = backward_diff(mz[2], nz, 2)
    shear_one = forward_diff(my[0], ny, 1) + forward_diff(mx[1], nx, 0)
    shear_two = forward_diff(mz[0], nz, 2) + forward_diff(mx[2], nx, 0)
    shear_three = forward_diff(mz[1], nz, 2) + forward_diff(my[2], ny, 1)
    dilation = rate_first + rate_second + rate_third
    grown = stress + time_step * jnp.stack(
        [
            lame_first * dilation + 2.0 * shear_modulus * rate_first,
            lame_first * dilation + 2.0 * shear_modulus * rate_second,
            lame_first * dilation + 2.0 * shear_modulus * rate_third,
            shear_modulus * shear_one,
            shear_modulus * shear_two,
            shear_modulus * shear_three,
        ]
    )
    strain_vals = strain_now.astype(jnp.float32)
    lame_kernel = lame_kernel + time_step * (strain_vals[0] + strain_vals[1] + strain_vals[2]) * dilation
    shear_kernel = shear_kernel + 2.0 * time_step * (
        strain_vals[0] * rate_first
        + strain_vals[1] * rate_second
        + strain_vals[2] * rate_third
        + strain_vals[3] * shear_one
        + strain_vals[4] * shear_two
        + strain_vals[5] * shear_three
    )
    return (moved, grown, lame_kernel, shear_kernel)


def pair_kernel(block, samples, station_ref, mine_ref, other_ref, out_ref, acc_ref, toward_ref):
    step = pl.program_id(0)

    @pl.when(step == 0)
    def _():
        acc_ref[...] = jnp.zeros_like(acc_ref)

    mine_vals = mine_ref[...].astype(jnp.float32)
    other_vals = other_ref[...].astype(jnp.float32)
    mine_sq = jnp.sum(jnp.sum(mine_vals * mine_vals, axis=2, keepdims=True), axis=1, keepdims=True)
    other_sq = jnp.sum(jnp.sum(other_vals * other_vals, axis=2, keepdims=True), axis=1, keepdims=True)
    cross = jnp.sum(jnp.sum(mine_vals * other_vals, axis=2, keepdims=True), axis=1, keepdims=True)
    mine_norm = jnp.sqrt(mine_sq / samples + epsilon)
    other_norm = jnp.sqrt(other_sq / samples + epsilon)
    corr = (cross / samples) / (mine_norm * other_norm)
    toward = other_vals / other_norm - corr * (mine_vals / mine_norm)
    toward_ref[...] = toward.astype(jnp.bfloat16).astype(jnp.float32)

    ways = acc_ref.shape[0]

    def add_some(i, carry):
        for way in range(ways):
            slot = i * ways + way
            target = station_ref[step * block + slot]
            acc_ref[way, target] = acc_ref[way, target] + toward_ref[slot]
        return carry

    lax.fori_loop(0, block // ways, add_some, 0)

    @pl.when(step == pl.num_programs(0) - 1)
    def _():
        stations = out_ref.shape[0]
        total = acc_ref[0, :stations]
        for way in range(1, ways):
            total = total + acc_ref[way, :stations]
        out_ref[...] = total


def pair_sums(targets, mine, other, stations):
    slots, rows, lanes = mine.shape
    block = 64
    samples = rows * lanes
    spec = pl.BlockSpec((block, rows, lanes), lambda g, t: (g, 0, 0))
    return pl.pallas_call(
        functools.partial(pair_kernel, block, float(samples)),
        grid_spec=pltpu.PrefetchScalarGridSpec(
            num_scalar_prefetch=1,
            grid=(slots // block,),
            in_specs=[spec, spec],
            out_specs=pl.BlockSpec((stations, rows, lanes), lambda g, t: (0, 0, 0)),
            scratch_shapes=[
                pltpu.VMEM((4, stations + 1, rows, lanes), jnp.float32),
                pltpu.VMEM((block, rows, lanes), jnp.float32),
            ],
        ),
        out_shape=jax.ShapeDtypeStruct((stations, rows, lanes), jnp.float32),
        compiler_params=pltpu.CompilerParams(dimension_semantics=("arbitrary",)),
        cost_estimate=pl.CostEstimate(flops=20 * slots * samples, transcendentals=0, bytes_accessed=4 * slots * samples),
    )(targets, mine, other)


def station_part(residuals, station_cell, station_pairs, cells_first, cells_second, step_count):
    stations_here = residuals.shape[0]
    samples = residuals.shape[1]
    devices = lax.axis_size(("gx", "gy"))
    pair_rows = station_pairs.shape[0] // devices
    me = lax.axis_index(("gx", "gy"))
    own = lax.dynamic_slice_in_dim(station_pairs, me * pair_rows, pair_rows, 0)
    first_local = own[:, 0] - me * stations_here
    dest = own[:, 1] // stations_here
    order = jnp.arange(pair_rows)
    same = (dest[:, None] == dest[None, :]) & (order[None, :] < order[:, None])
    rank = jnp.sum(same.astype(jnp.int32), axis=1)
    device_ids = jnp.arange(devices)
    pick_own = (dest[None, :, None] == device_ids[:, None, None]) & (rank[None, :, None] == jnp.arange(2)[None, None, :])
    own_station = jnp.sum(jnp.where(pick_own, first_local[None, :, None] + 1, 0), axis=1) - 1
    blocks = station_pairs.reshape(devices, pair_rows, 2)
    hit = (blocks[:, :, 1] // stations_here == me).astype(jnp.int32)
    before = jnp.cumsum(hit, axis=1) - hit
    pick_in = (hit[:, :, None] > 0) & (before[:, :, None] == jnp.arange(2)[None, None, :])
    in_station = jnp.sum(jnp.where(pick_in, (blocks[:, :, 1] % stations_here)[:, :, None] + 1, 0), axis=1) - 1
    slot_station = jnp.concatenate([own_station, in_station], axis=1)
    lanes = 128
    rows = residuals.reshape(stations_here, samples // lanes, lanes)
    padded_rows = jnp.concatenate([rows, jnp.zeros((1,) + rows.shape[1:], rows.dtype)], axis=0)
    send = padded_rows[jnp.where(slot_station >= 0, slot_station, stations_here)]
    recv = lax.all_to_all(send, ("gx", "gy"), split_axis=0, concat_axis=0, tiled=True)
    mine_station = jnp.concatenate([slot_station[:, 2:4], slot_station[:, 0:2]], axis=1)
    mine = padded_rows[jnp.where(mine_station >= 0, mine_station, stations_here)]
    slots = devices * 4
    targets = jnp.where(mine_station >= 0, mine_station, stations_here).reshape(slots)
    adjoint3 = pair_sums(
        targets, mine.reshape(slots, samples // lanes, lanes), recv.reshape(slots, samples // lanes, lanes), stations_here
    )
    adjoint = adjoint3.reshape(stations_here, samples)
    last = adjoint3[:, samples // lanes - 1, lanes - step_count :]
    tail = last
    cells_hit = (station_cell[:, None] == jnp.arange(cells_first * cells_second)[None, :]).astype(jnp.float32)
    surfaces = jnp.stack(
        [
            jnp.sum(cells_hit * tail[:, step_count - 1 - window_step][:, None], axis=0).reshape(cells_first, cells_second)
            for window_step in range(step_count)
        ]
    )
    return adjoint, surfaces


def shards(velocity, stress, lame_first, shear_modulus, buoyancy, forward_strain, lame_accum, shear_accum, residuals, station_cell, station_pairs):
    step_count = forward_strain.shape[0] // 6
    adjoint, surfaces = station_part(residuals, station_cell, station_pairs, velocity.shape[1], velocity.shape[2], step_count)
    for window_step in range(step_count):
        strain_now = forward_strain[6 * window_step : 6 * window_step + 6]
        velocity, stress, lame_accum, shear_accum = advance(
            velocity, stress, lame_first, shear_modulus, buoyancy, strain_now, surfaces[window_step], lame_accum, shear_accum
        )
    return (velocity, stress, lame_accum, shear_accum, adjoint)


def solution(mesh):
    return jax.shard_map(
        shards,
        mesh=mesh,
        in_specs=(
            P(None, "gx", "gy", None),
            P(None, "gx", "gy", None),
            P("gx", "gy", None),
            P("gx", "gy", None),
            P("gx", "gy", None),
            P(None, "gx", "gy", None),
            P("gx", "gy", None),
            P("gx", "gy", None),
            P(("gx", "gy"), None),
            P(("gx", "gy")),
            P(),
        ),
        out_specs=(
            P(None, "gx", "gy", None),
            P(None, "gx", "gy", None),
            P("gx", "gy", None),
            P("gx", "gy", None),
            P(("gx", "gy"), None),
        ),
        check_vma=False,
    )
```

```python
import functools

import jax
import jax.numpy as jnp
from jax import lax
from jax.sharding import PartitionSpec as P
from jax.experimental import pallas as pl
from jax.experimental.pallas import tpu as pltpu

near_weight = 9.0 / 8.0
far_weight = -1.0 / 24.0
time_step = 0.25
epsilon = 1e-06


def shifted(padded, start, length, axis):
    return lax.slice_in_dim(padded, start, start + length, axis=axis)


def backward_diff(padded, length, axis):
    return near_weight * (
        shifted(padded, 2, length, axis) - shifted(padded, 1, length, axis)
    ) + far_weight * (shifted(padded, 3, length, axis) - shifted(padded, 0, length, axis))


def forward_diff(padded, length, axis):
    return near_weight * (
        shifted(padded, 3, length, axis) - shifted(padded, 2, length, axis)
    ) + far_weight * (shifted(padded, 4, length, axis) - shifted(padded, 1, length, axis))


def halo_pad(block, axis, dim, width=2):
    count = lax.axis_size(axis)
    forward = [(i, i + 1) for i in range(count - 1)]
    backward = [(i + 1, i) for i in range(count - 1)]
    size = block.shape[dim]
    low = lax.ppermute(lax.slice_in_dim(block, size - width, size, axis=dim), axis, forward)
    high = lax.ppermute(lax.slice_in_dim(block, 0, width, axis=dim), axis, backward)
    return jnp.concatenate([low, block, high], axis=dim)


def z_pad(block):
    pads = [(0, 0)] * (block.ndim - 1) + [(2, 2)]
    return jnp.pad(block, pads)


def advance(velocity, stress, lame_first, shear_modulus, buoyancy, strain_now, surface, lame_kernel, shear_kernel):
    nx = velocity.shape[1]
    ny = velocity.shape[2]
    nz = velocity.shape[3]
    sx = halo_pad(jnp.stack([stress[0], stress[3], stress[4]]), "gx", 1)
    sy = halo_pad(jnp.stack([stress[3], stress[1], stress[5]]), "gy", 2)
    sz = z_pad(jnp.stack([stress[4], stress[5], stress[2]]))
    force_first = forward_diff(sx[0], nx, 0) + backward_diff(sy[0], ny, 1) + backward_diff(sz[0], nz, 2)
    force_second = backward_diff(sx[1], nx, 0) + forward_diff(sy[1], ny, 1) + backward_diff(sz[1], nz, 2)
    force_third = backward_diff(sx[2], nx, 0) + backward_diff(sy[2], ny, 1) + forward_diff(sz[2], nz, 2)
    force_third = force_third.at[:, :, 0].add(surface)
    moved = velocity + time_step * buoyancy[None] * jnp.stack([force_first, force_second, force_third])
    mx = halo_pad(moved, "gx", 1)
    my = halo_pad(moved, "gy", 2)
    mz = z_pad(moved)
    rate_first = backward_diff(mx[0], nx, 0)
    rate_second = backward_diff(my[1], ny, 1)
    rate_third = backward_diff(mz[2], nz, 2)
    shear_one = forward_diff(my[0], ny, 1) + forward_diff(mx[1], nx, 0)
    shear_two = forward_diff(mz[0], nz, 2) + forward_diff(mx[2], nx, 0)
    shear_three = forward_diff(mz[1], nz, 2) + forward_diff(my[2], ny, 1)
    dilation = rate_first + rate_second + rate_third
    grown = stress + time_step * jnp.stack(
        [
            lame_first * dilation + 2.0 * shear_modulus * rate_first,
            lame_first * dilation + 2.0 * shear_modulus * rate_second,
            lame_first * dilation + 2.0 * shear_modulus * rate_third,
            shear_modulus * shear_one,
            shear_modulus * shear_two,
            shear_modulus * shear_three,
        ]
    )
    strain_vals = strain_now.astype(jnp.float32)
    lame_kernel = lame_kernel + time_step * (strain_vals[0] + strain_vals[1] + strain_vals[2]) * dilation
    shear_kernel = shear_kernel + 2.0 * time_step * (
        strain_vals[0] * rate_first
        + strain_vals[1] * rate_second
        + strain_vals[2] * rate_third
        + strain_vals[3] * shear_one
        + strain_vals[4] * shear_two
        + strain_vals[5] * shear_three
    )
    return (moved, grown, lame_kernel, shear_kernel)


def pair_kernel(block, samples, station_ref, mine_ref, other_ref, out_ref, acc_ref, toward_ref):
    step = pl.program_id(0)

    @pl.when(step == 0)
    def _():
        acc_ref[...] = jnp.zeros_like(acc_ref)

    mine_vals = mine_ref[...].astype(jnp.float32)
    other_vals = other_ref[...].astype(jnp.float32)
    mine_sq = jnp.sum(jnp.sum(mine_vals * mine_vals, axis=1, keepdims=True), axis=2, keepdims=True)
    other_sq = jnp.sum(jnp.sum(other_vals * other_vals, axis=1, keepdims=True), axis=2, keepdims=True)
    cross = jnp.sum(jnp.sum(mine_vals * other_vals, axis=1, keepdims=True), axis=2, keepdims=True)
    mine_norm = jnp.sqrt(mine_sq / samples + epsilon)
    other_norm = jnp.sqrt(other_sq / samples + epsilon)
    corr = (cross / samples) / (mine_norm * other_norm)
    toward = other_vals / other_norm - corr * (mine_vals / mine_norm)
    toward_ref[...] = toward.astype(jnp.bfloat16).astype(jnp.float32)

    ways = acc_ref.shape[0]

    def add_some(i, carry):
        for way in range(ways):
            slot = i * ways + way
            target = station_ref[step * block + slot]
            acc_ref[way, target] = acc_ref[way, target] + toward_ref[slot]
        return carry

    lax.fori_loop(0, block // ways, add_some, 0)

    @pl.when(step == pl.num_programs(0) - 1)
    def _():
        stations = out_ref.shape[0]
        total = acc_ref[0, :stations]
        for way in range(1, ways):
            total = total + acc_ref[way, :stations]
        out_ref[...] = total


def pair_sums(targets, mine, other, stations):
    slots, rows, lanes = mine.shape
    block = 64
    samples = rows * lanes
    spec = pl.BlockSpec((block, rows, lanes), lambda g, t: (g, 0, 0))
    return pl.pallas_call(
        functools.partial(pair_kernel, block, float(samples)),
        grid_spec=pltpu.PrefetchScalarGridSpec(
            num_scalar_prefetch=1,
            grid=(slots // block,),
            in_specs=[spec, spec],
            out_specs=pl.BlockSpec((stations, rows, lanes), lambda g, t: (0, 0, 0)),
            scratch_shapes=[
                pltpu.VMEM((4, stations + 1, rows, lanes), jnp.float32),
                pltpu.VMEM((block, rows, lanes), jnp.float32),
            ],
        ),
        out_shape=jax.ShapeDtypeStruct((stations, rows, lanes), jnp.float32),
        compiler_params=pltpu.CompilerParams(dimension_semantics=("arbitrary",)),
        cost_estimate=pl.CostEstimate(flops=20 * slots * samples, transcendentals=0, bytes_accessed=4 * slots * samples),
    )(targets, mine, other)


def station_part(residuals, station_cell, station_pairs, cells_first, cells_second, step_count):
    stations_here = residuals.shape[0]
    samples = residuals.shape[1]
    devices = lax.axis_size(("gx", "gy"))
    pair_rows = station_pairs.shape[0] // devices
    me = lax.axis_index(("gx", "gy"))
    own = lax.dynamic_slice_in_dim(station_pairs, me * pair_rows, pair_rows, 0)
    first_local = own[:, 0] - me * stations_here
    dest = own[:, 1] // stations_here
    order = jnp.arange(pair_rows)
    same = (dest[:, None] == dest[None, :]) & (order[None, :] < order[:, None])
    rank = jnp.sum(same.astype(jnp.int32), axis=1)
    device_ids = jnp.arange(devices)
    pick_own = (dest[None, :, None] == device_ids[:, None, None]) & (rank[None, :, None] == jnp.arange(2)[None, None, :])
    own_station = jnp.sum(jnp.where(pick_own, first_local[None, :, None] + 1, 0), axis=1) - 1
    blocks = station_pairs.reshape(devices, pair_rows, 2)
    hit = (blocks[:, :, 1] // stations_here == me).astype(jnp.int32)
    before = jnp.cumsum(hit, axis=1) - hit
    pick_in = (hit[:, :, None] > 0) & (before[:, :, None] == jnp.arange(2)[None, None, :])
    in_station = jnp.sum(jnp.where(pick_in, (blocks[:, :, 1] % stations_here)[:, :, None] + 1, 0), axis=1) - 1
    slot_station = jnp.concatenate([own_station, in_station], axis=1)
    lanes = 128
    rows = residuals.reshape(stations_here, samples // lanes, lanes)
    padded_rows = jnp.concatenate([rows, jnp.zeros((1,) + rows.shape[1:], rows.dtype)], axis=0)
    send = padded_rows[jnp.where(slot_station >= 0, slot_station, stations_here)]
    recv = lax.all_to_all(send, ("gx", "gy"), split_axis=0, concat_axis=0, tiled=True)
    mine_station = jnp.concatenate([slot_station[:, 2:4], slot_station[:, 0:2]], axis=1)
    mine = padded_rows[jnp.where(mine_station >= 0, mine_station, stations_here)]
    slots = devices * 4
    targets = jnp.where(mine_station >= 0, mine_station, stations_here).reshape(slots)
    adjoint3 = pair_sums(
        targets, mine.reshape(slots, samples // lanes, lanes), recv.reshape(slots, samples // lanes, lanes), stations_here
    )
    adjoint = adjoint3.reshape(stations_here, samples)
    last = adjoint3[:, samples // lanes - 1, lanes - step_count :]
    tail = last
    cells_hit = (station_cell[:, None] == jnp.arange(cells_first * cells_second)[None, :]).astype(jnp.float32)
    surfaces = jnp.stack(
        [
            jnp.sum(cells_hit * tail[:, step_count - 1 - window_step][:, None], axis=0).reshape(cells_first, cells_second)
            for window_step in range(step_count)
        ]
    )
    return adjoint, surfaces


def shards(velocity, stress, lame_first, shear_modulus, buoyancy, forward_strain, lame_accum, shear_accum, residuals, station_cell, station_pairs):
    step_count = forward_strain.shape[0] // 6
    adjoint, surfaces = station_part(residuals, station_cell, station_pairs, velocity.shape[1], velocity.shape[2], step_count)
    for window_step in range(step_count):
        strain_now = forward_strain[6 * window_step : 6 * window_step + 6]
        velocity, stress, lame_accum, shear_accum = advance(
            velocity, stress, lame_first, shear_modulus, buoyancy, strain_now, surfaces[window_step], lame_accum, shear_accum
        )
    return (velocity, stress, lame_accum, shear_accum, adjoint)


def solution(mesh):
    return jax.shard_map(
        shards,
        mesh=mesh,
        in_specs=(
            P(None, "gx", "gy", None),
            P(None, "gx", "gy", None),
            P("gx", "gy", None),
            P("gx", "gy", None),
            P("gx", "gy", None),
            P(None, "gx", "gy", None),
            P("gx", "gy", None),
            P("gx", "gy", None),
            P(("gx", "gy"), None),
            P(("gx", "gy")),
            P(),
        ),
        out_specs=(
            P(None, "gx", "gy", None),
            P(None, "gx", "gy", None),
            P("gx", "gy", None),
            P("gx", "gy", None),
            P(("gx", "gy"), None),
        ),
        check_vma=False,
    )
```

```python
import functools

import jax
import jax.numpy as jnp
from jax import lax
from jax.sharding import PartitionSpec as P
from jax.experimental import pallas as pl
from jax.experimental.pallas import tpu as pltpu

near_weight = 9.0 / 8.0
far_weight = -1.0 / 24.0
time_step = 0.25
epsilon = 1e-06


def shifted(padded, start, length, axis):
    return lax.slice_in_dim(padded, start, start + length, axis=axis)


def backward_diff(padded, length, axis):
    return near_weight * (
        shifted(padded, 2, length, axis) - shifted(padded, 1, length, axis)
    ) + far_weight * (shifted(padded, 3, length, axis) - shifted(padded, 0, length, axis))


def forward_diff(padded, length, axis):
    return near_weight * (
        shifted(padded, 3, length, axis) - shifted(padded, 2, length, axis)
    ) + far_weight * (shifted(padded, 4, length, axis) - shifted(padded, 1, length, axis))


def halo_pad(block, axis, dim, width=2):
    count = lax.axis_size(axis)
    forward = [(i, i + 1) for i in range(count - 1)]
    backward = [(i + 1, i) for i in range(count - 1)]
    size = block.shape[dim]
    low = lax.ppermute(lax.slice_in_dim(block, size - width, size, axis=dim), axis, forward)
    high = lax.ppermute(lax.slice_in_dim(block, 0, width, axis=dim), axis, backward)
    return jnp.concatenate([low, block, high], axis=dim)


def z_pad(block):
    pads = [(0, 0)] * (block.ndim - 1) + [(2, 2)]
    return jnp.pad(block, pads)


def advance(velocity, stress, lame_first, shear_modulus, buoyancy, strain_now, surface, lame_kernel, shear_kernel):
    nx = velocity.shape[1]
    ny = velocity.shape[2]
    nz = velocity.shape[3]
    sx = halo_pad(jnp.stack([stress[0], stress[3], stress[4]]), "gx", 1)
    sy = halo_pad(jnp.stack([stress[3], stress[1], stress[5]]), "gy", 2)
    sz = z_pad(jnp.stack([stress[4], stress[5], stress[2]]))
    force_first = forward_diff(sx[0], nx, 0) + backward_diff(sy[0], ny, 1) + backward_diff(sz[0], nz, 2)
    force_second = backward_diff(sx[1], nx, 0) + forward_diff(sy[1], ny, 1) + backward_diff(sz[1], nz, 2)
    force_third = backward_diff(sx[2], nx, 0) + backward_diff(sy[2], ny, 1) + forward_diff(sz[2], nz, 2)
    force_third = force_third.at[:, :, 0].add(surface)
    moved = velocity + time_step * buoyancy[None] * jnp.stack([force_first, force_second, force_third])
    mx = halo_pad(moved, "gx", 1)
    my = halo_pad(moved, "gy", 2)
    mz = z_pad(moved)
    rate_first = backward_diff(mx[0], nx, 0)
    rate_second = backward_diff(my[1], ny, 1)
    rate_third = backward_diff(mz[2], nz, 2)
    shear_one = forward_diff(my[0], ny, 1) + forward_diff(mx[1], nx, 0)
    shear_two = forward_diff(mz[0], nz, 2) + forward_diff(mx[2], nx, 0)
    shear_three = forward_diff(mz[1], nz, 2) + forward_diff(my[2], ny, 1)
    dilation = rate_first + rate_second + rate_third
    grown = stress + time_step * jnp.stack(
        [
            lame_first * dilation + 2.0 * shear_modulus * rate_first,
            lame_first * dilation + 2.0 * shear_modulus * rate_second,
            lame_first * dilation + 2.0 * shear_modulus * rate_third,
            shear_modulus * shear_one,
            shear_modulus * shear_two,
            shear_modulus * shear_three,
        ]
    )
    strain_vals = strain_now.astype(jnp.float32)
    lame_kernel = lame_kernel + time_step * (strain_vals[0] + strain_vals[1] + strain_vals[2]) * dilation
    shear_kernel = shear_kernel + 2.0 * time_step * (
        strain_vals[0] * rate_first
        + strain_vals[1] * rate_second
        + strain_vals[2] * rate_third
        + strain_vals[3] * shear_one
        + strain_vals[4] * shear_two
        + strain_vals[5] * shear_three
    )
    return (moved, grown, lame_kernel, shear_kernel)


def stats_kernel(mine_ref, other_ref, mine_out, other_out, cross_out):
    mine_vals = mine_ref[...].astype(jnp.float32)
    other_vals = other_ref[...].astype(jnp.float32)
    shape = mine_out.shape
    for values, out in ((mine_vals * mine_vals, mine_out), (other_vals * other_vals, other_out), (mine_vals * other_vals, cross_out)):
        total = jnp.sum(jnp.sum(values, axis=1, keepdims=True), axis=2, keepdims=True)
        out[...] = jnp.broadcast_to(total, shape)


def row_stats(mine, other):
    slots, rows, lanes = mine.shape
    block = 64
    spec = pl.BlockSpec((block, rows, lanes), lambda g: (g, 0, 0))
    small = pl.BlockSpec((block, 1, lanes), lambda g: (g, 0, 0))
    shape = jax.ShapeDtypeStruct((slots, 1, lanes), jnp.float32)
    return pl.pallas_call(
        stats_kernel,
        grid=(slots // block,),
        in_specs=[spec, spec],
        out_specs=[small, small, small],
        out_shape=[shape, shape, shape],
        compiler_params=pltpu.CompilerParams(dimension_semantics=("arbitrary",)),
        cost_estimate=pl.CostEstimate(flops=6 * slots * rows * lanes, transcendentals=0, bytes_accessed=4 * slots * rows * lanes),
    )(mine, other)


def pair_kernel(block, station_ref, mine_ref, other_ref, other_scale_ref, mine_scale_ref, out_ref, acc_ref, toward_ref):
    step = pl.program_id(0)

    @pl.when(step == 0)
    def _():
        acc_ref[...] = jnp.zeros_like(acc_ref)

    mine_vals = mine_ref[...].astype(jnp.float32)
    other_vals = other_ref[...].astype(jnp.float32)
    toward = other_vals * other_scale_ref[...] - mine_scale_ref[...] * mine_vals
    toward_ref[...] = toward.astype(jnp.bfloat16).astype(jnp.float32)
    ways = acc_ref.shape[0]

    def add_some(i, carry):
        for way in range(ways):
            slot = i * ways + way
            target = station_ref[step * block + slot]
            acc_ref[way, target] = acc_ref[way, target] + toward_ref[slot]
        return carry

    lax.fori_loop(0, block // ways, add_some, 0)

    @pl.when(step == pl.num_programs(0) - 1)
    def _():
        stations = out_ref.shape[0]
        total = acc_ref[0, :stations]
        for way in range(1, ways):
            total = total + acc_ref[way, :stations]
        out_ref[...] = total


def pair_sums(targets, mine, other, other_scale, mine_scale, stations):
    slots, rows, lanes = mine.shape
    block = 64
    samples = rows * lanes
    spec = pl.BlockSpec((block, rows, lanes), lambda g, t: (g, 0, 0))
    small = pl.BlockSpec((block, 1, lanes), lambda g, t: (g, 0, 0))
    return pl.pallas_call(
        functools.partial(pair_kernel, block),
        grid_spec=pltpu.PrefetchScalarGridSpec(
            num_scalar_prefetch=1,
            grid=(slots // block,),
            in_specs=[spec, spec, small, small],
            out_specs=pl.BlockSpec((stations, rows, lanes), lambda g, t: (0, 0, 0)),
            scratch_shapes=[
                pltpu.VMEM((4, stations + 1, rows, lanes), jnp.float32),
                pltpu.VMEM((block, rows, lanes), jnp.float32),
            ],
        ),
        out_shape=jax.ShapeDtypeStruct((stations, rows, lanes), jnp.float32),
        compiler_params=pltpu.CompilerParams(dimension_semantics=("arbitrary",)),
        cost_estimate=pl.CostEstimate(flops=8 * slots * samples, transcendentals=0, bytes_accessed=4 * slots * samples),
    )(targets, mine, other, other_scale, mine_scale)


def station_part(residuals, station_cell, station_pairs, cells_first, cells_second, step_count):
    stations_here = residuals.shape[0]
    samples = residuals.shape[1]
    devices = lax.axis_size(("gx", "gy"))
    pair_rows = station_pairs.shape[0] // devices
    me = lax.axis_index(("gx", "gy"))
    own = lax.dynamic_slice_in_dim(station_pairs, me * pair_rows, pair_rows, 0)
    first_local = own[:, 0] - me * stations_here
    dest = own[:, 1] // stations_here
    order = jnp.arange(pair_rows)
    same = (dest[:, None] == dest[None, :]) & (order[None, :] < order[:, None])
    rank = jnp.sum(same.astype(jnp.int32), axis=1)
    device_ids = jnp.arange(devices)
    pick_own = (dest[None, :, None] == device_ids[:, None, None]) & (rank[None, :, None] == jnp.arange(2)[None, None, :])
    own_station = jnp.sum(jnp.where(pick_own, first_local[None, :, None] + 1, 0), axis=1) - 1
    blocks = station_pairs.reshape(devices, pair_rows, 2)
    hit = (blocks[:, :, 1] // stations_here == me).astype(jnp.int32)
    before = jnp.cumsum(hit, axis=1) - hit
    pick_in = (hit[:, :, None] > 0) & (before[:, :, None] == jnp.arange(2)[None, None, :])
    in_station = jnp.sum(jnp.where(pick_in, (blocks[:, :, 1] % stations_here)[:, :, None] + 1, 0), axis=1) - 1
    slot_station = jnp.concatenate([own_station, in_station], axis=1)
    lanes = 128
    rows = residuals.reshape(stations_here, samples // lanes, lanes)
    padded_rows = jnp.concatenate([rows, jnp.zeros((1,) + rows.shape[1:], rows.dtype)], axis=0)
    send = padded_rows[jnp.where(slot_station >= 0, slot_station, stations_here)]
    recv = lax.all_to_all(send, ("gx", "gy"), split_axis=0, concat_axis=0, tiled=True)
    mine_station = jnp.concatenate([slot_station[:, 2:4], slot_station[:, 0:2]], axis=1)
    mine = padded_rows[jnp.where(mine_station >= 0, mine_station, stations_here)]
    slots = devices * 4
    targets = jnp.where(mine_station >= 0, mine_station, stations_here).reshape(slots)
    mine_rows = mine.reshape(slots, samples // lanes, lanes)
    other_rows = recv.reshape(slots, samples // lanes, lanes)
    mine_sq, other_sq, cross = row_stats(mine_rows, other_rows)
    mine_norm = jnp.sqrt(mine_sq / samples + epsilon)
    other_norm = jnp.sqrt(other_sq / samples + epsilon)
    corr = (cross / samples) / (mine_norm * other_norm)
    other_scale = 1.0 / other_norm
    mine_scale = corr / mine_norm
    adjoint3 = pair_sums(targets, mine_rows, other_rows, other_scale, mine_scale, stations_here)
    adjoint = adjoint3.reshape(stations_here, samples)
    end_other = other_rows[:, -1, lanes - step_count :].astype(jnp.float32)
    end_mine = mine_rows[:, -1, lanes - step_count :].astype(jnp.float32)
    end_toward = (end_other * other_scale[:, 0, :1] - mine_scale[:, 0, :1] * end_mine).astype(jnp.bfloat16).astype(jnp.float32)
    slot_hits = (targets[:, None] == jnp.arange(stations_here)[None, :]).astype(jnp.float32)
    tail = jnp.dot(slot_hits.T, end_toward, precision=lax.Precision.HIGHEST)
    cells_hit = (station_cell[:, None] == jnp.arange(cells_first * cells_second)[None, :]).astype(jnp.float32)
    surfaces = jnp.stack(
        [
            jnp.sum(cells_hit * tail[:, step_count - 1 - window_step][:, None], axis=0).reshape(cells_first, cells_second)
            for window_step in range(step_count)
        ]
    )
    return adjoint, surfaces


def shards(velocity, stress, lame_first, shear_modulus, buoyancy, forward_strain, lame_accum, shear_accum, residuals, station_cell, station_pairs):
    step_count = forward_strain.shape[0] // 6
    adjoint, surfaces = station_part(residuals, station_cell, station_pairs, velocity.shape[1], velocity.shape[2], step_count)
    for window_step in range(step_count):
        strain_now = forward_strain[6 * window_step : 6 * window_step + 6]
        velocity, stress, lame_accum, shear_accum = advance(
            velocity, stress, lame_first, shear_modulus, buoyancy, strain_now, surfaces[window_step], lame_accum, shear_accum
        )
    return (velocity, stress, lame_accum, shear_accum, adjoint)


def solution(mesh):
    return jax.shard_map(
        shards,
        mesh=mesh,
        in_specs=(
            P(None, "gx", "gy", None),
            P(None, "gx", "gy", None),
            P("gx", "gy", None),
            P("gx", "gy", None),
            P("gx", "gy", None),
            P(None, "gx", "gy", None),
            P("gx", "gy", None),
            P("gx", "gy", None),
            P(("gx", "gy"), None),
            P(("gx", "gy")),
            P(),
        ),
        out_specs=(
            P(None, "gx", "gy", None),
            P(None, "gx", "gy", None),
            P("gx", "gy", None),
            P("gx", "gy", None),
            P(("gx", "gy"), None),
        ),
        check_vma=False,
    )
```

```python
import functools

import jax
import jax.numpy as jnp
from jax import lax
from jax.sharding import PartitionSpec as P
from jax.experimental import pallas as pl
from jax.experimental.pallas import tpu as pltpu

near_weight = 9.0 / 8.0
far_weight = -1.0 / 24.0
time_step = 0.25
epsilon = 1e-06


def shifted(padded, start, length, axis):
    return lax.slice_in_dim(padded, start, start + length, axis=axis)


def backward_diff(padded, length, axis):
    return near_weight * (
        shifted(padded, 2, length, axis) - shifted(padded, 1, length, axis)
    ) + far_weight * (shifted(padded, 3, length, axis) - shifted(padded, 0, length, axis))


def forward_diff(padded, length, axis):
    return near_weight * (
        shifted(padded, 3, length, axis) - shifted(padded, 2, length, axis)
    ) + far_weight * (shifted(padded, 4, length, axis) - shifted(padded, 1, length, axis))


def halo_pad(block, axis, dim, width=2):
    count = lax.axis_size(axis)
    forward = [(i, i + 1) for i in range(count - 1)]
    backward = [(i + 1, i) for i in range(count - 1)]
    size = block.shape[dim]
    low = lax.ppermute(lax.slice_in_dim(block, size - width, size, axis=dim), axis, forward)
    high = lax.ppermute(lax.slice_in_dim(block, 0, width, axis=dim), axis, backward)
    return jnp.concatenate([low, block, high], axis=dim)


def z_pad(block):
    pads = [(0, 0)] * (block.ndim - 1) + [(2, 2)]
    return jnp.pad(block, pads)


def exchange(block):
    wide_x = halo_pad(block[0], "gx", 1)
    wide_y = halo_pad(block[1], "gy", 2)
    return wide_x, wide_y


def advance(velocity, stress, lame_first, shear_modulus, buoyancy, strain_now, surface, lame_kernel, shear_kernel):
    nx = velocity.shape[1]
    ny = velocity.shape[2]
    nz = velocity.shape[3]
    sx, sy = exchange((jnp.stack([stress[0], stress[3], stress[4]]), jnp.stack([stress[3], stress[1], stress[5]])))
    sz = z_pad(jnp.stack([stress[4], stress[5], stress[2]]))
    force_first = forward_diff(sx[0], nx, 0) + backward_diff(sy[0], ny, 1) + backward_diff(sz[0], nz, 2)
    force_second = backward_diff(sx[1], nx, 0) + forward_diff(sy[1], ny, 1) + backward_diff(sz[1], nz, 2)
    force_third = backward_diff(sx[2], nx, 0) + backward_diff(sy[2], ny, 1) + forward_diff(sz[2], nz, 2)
    force_third = force_third.at[:, :, 0].add(surface)
    moved = velocity + time_step * buoyancy[None] * jnp.stack([force_first, force_second, force_third])
    mx, my = exchange((moved, moved))
    mz = z_pad(moved)
    rate_first = backward_diff(mx[0], nx, 0)
    rate_second = backward_diff(my[1], ny, 1)
    rate_third = backward_diff(mz[2], nz, 2)
    shear_one = forward_diff(my[0], ny, 1) + forward_diff(mx[1], nx, 0)
    shear_two = forward_diff(mz[0], nz, 2) + forward_diff(mx[2], nx, 0)
    shear_three = forward_diff(mz[1], nz, 2) + forward_diff(my[2], ny, 1)
    dilation = rate_first + rate_second + rate_third
    grown = stress + time_step * jnp.stack(
        [
            lame_first * dilation + 2.0 * shear_modulus * rate_first,
            lame_first * dilation + 2.0 * shear_modulus * rate_second,
            lame_first * dilation + 2.0 * shear_modulus * rate_third,
            shear_modulus * shear_one,
            shear_modulus * shear_two,
            shear_modulus * shear_three,
        ]
    )
    strain_vals = strain_now.astype(jnp.float32)
    lame_kernel = lame_kernel + time_step * (strain_vals[0] + strain_vals[1] + strain_vals[2]) * dilation
    shear_kernel = shear_kernel + 2.0 * time_step * (
        strain_vals[0] * rate_first
        + strain_vals[1] * rate_second
        + strain_vals[2] * rate_third
        + strain_vals[3] * shear_one
        + strain_vals[4] * shear_two
        + strain_vals[5] * shear_three
    )
    return (moved, grown, lame_kernel, shear_kernel)


def pair_kernel(samples, mine_ref, other_ref, hits_ref, out_ref, toward_ref):
    step = pl.program_id(0)

    @pl.when(step == 0)
    def _():
        out_ref[...] = jnp.zeros_like(out_ref)

    mine_vals = mine_ref[...].astype(jnp.float32)
    other_vals = other_ref[...].astype(jnp.float32)
    mine_sq = jnp.sum(jnp.sum(mine_vals * mine_vals, axis=1, keepdims=True), axis=2, keepdims=True)
    other_sq = jnp.sum(jnp.sum(other_vals * other_vals, axis=1, keepdims=True), axis=2, keepdims=True)
    cross = jnp.sum(jnp.sum(mine_vals * other_vals, axis=1, keepdims=True), axis=2, keepdims=True)
    mine_norm = jnp.sqrt(mine_sq / samples + epsilon)
    other_norm = jnp.sqrt(other_sq / samples + epsilon)
    corr = (cross / samples) / (mine_norm * other_norm)
    other_scale = 1.0 / other_norm
    mine_scale = corr / mine_norm
    toward = other_vals * other_scale - mine_scale * mine_vals
    block, rows, lanes = toward.shape
    toward_ref[...] = toward.astype(jnp.bfloat16).astype(jnp.float32).reshape(block * rows, lanes)
    hits = hits_ref[...]
    for row in range(rows):
        part = toward_ref[pl.ds(row, block, stride=rows), :]
        out_ref[row] = out_ref[row] + jnp.dot(hits, part, preferred_element_type=jnp.float32)


def pair_sums(hits_t, mine, other, stations):
    slots, rows, lanes = mine.shape
    block = 128
    samples = rows * lanes
    spec = pl.BlockSpec((block, rows, lanes), lambda g: (g, 0, 0))
    return pl.pallas_call(
        functools.partial(pair_kernel, float(samples)),
        grid=(slots // block,),
        in_specs=[spec, spec, pl.BlockSpec((stations, block), lambda g: (0, g))],
        out_specs=pl.BlockSpec((rows, stations, lanes), lambda g: (0, 0, 0)),
        out_shape=jax.ShapeDtypeStruct((rows, stations, lanes), jnp.float32),
        scratch_shapes=[pltpu.VMEM((block * rows, lanes), jnp.float32)],
        compiler_params=pltpu.CompilerParams(dimension_semantics=("arbitrary",)),
        cost_estimate=pl.CostEstimate(flops=20 * slots * samples, transcendentals=0, bytes_accessed=4 * slots * samples),
    )(mine, other, hits_t)


def station_part(residuals, station_cell, station_pairs, cells_first, cells_second, step_count):
    stations_here = residuals.shape[0]
    samples = residuals.shape[1]
    devices = lax.axis_size(("gx", "gy"))
    pair_rows = station_pairs.shape[0] // devices
    me = lax.axis_index(("gx", "gy"))
    own = lax.dynamic_slice_in_dim(station_pairs, me * pair_rows, pair_rows, 0)
    first_local = own[:, 0] - me * stations_here
    dest = own[:, 1] // stations_here
    order = jnp.arange(pair_rows)
    same = (dest[:, None] == dest[None, :]) & (order[None, :] < order[:, None])
    rank = jnp.sum(same.astype(jnp.int32), axis=1)
    device_ids = jnp.arange(devices)
    pick_own = (dest[None, :, None] == device_ids[:, None, None]) & (rank[None, :, None] == jnp.arange(2)[None, None, :])
    own_station = jnp.sum(jnp.where(pick_own, first_local[None, :, None] + 1, 0), axis=1) - 1
    blocks = station_pairs.reshape(devices, pair_rows, 2)
    hit = (blocks[:, :, 1] // stations_here == me).astype(jnp.int32)
    before = jnp.cumsum(hit, axis=1) - hit
    pick_in = (hit[:, :, None] > 0) & (before[:, :, None] == jnp.arange(2)[None, None, :])
    in_station = jnp.sum(jnp.where(pick_in, (blocks[:, :, 1] % stations_here)[:, :, None] + 1, 0), axis=1) - 1
    slot_station = jnp.concatenate([own_station, in_station], axis=1)
    lanes = 128
    rows = residuals.reshape(stations_here, samples // lanes, lanes)
    padded_rows = jnp.concatenate([rows, jnp.zeros((1,) + rows.shape[1:], rows.dtype)], axis=0)
    send = padded_rows[jnp.where(slot_station >= 0, slot_station, stations_here)]
    recv = lax.all_to_all(send, ("gx", "gy"), split_axis=0, concat_axis=0, tiled=True)
    mine_station = jnp.concatenate([slot_station[:, 2:4], slot_station[:, 0:2]], axis=1)
    mine = padded_rows[jnp.where(mine_station >= 0, mine_station, stations_here)]
    slots = devices * 4
    hits_t = (jnp.arange(stations_here)[:, None] == mine_station.reshape(slots)[None, :]).astype(jnp.float32)
    by_row = pair_sums(
        hits_t, mine.reshape(slots, samples // lanes, lanes), recv.reshape(slots, samples // lanes, lanes), stations_here
    )
    adjoint = by_row.transpose(1, 0, 2).reshape(stations_here, samples)
    tail = by_row[-1, :, lanes - step_count :]
    cells_hit = (station_cell[:, None] == jnp.arange(cells_first * cells_second)[None, :]).astype(jnp.float32)
    surfaces = jnp.stack(
        [
            jnp.sum(cells_hit * tail[:, step_count - 1 - window_step][:, None], axis=0).reshape(cells_first, cells_second)
            for window_step in range(step_count)
        ]
    )
    return adjoint, surfaces


def shards(velocity, stress, lame_first, shear_modulus, buoyancy, forward_strain, lame_accum, shear_accum, residuals, station_cell, station_pairs):
    step_count = forward_strain.shape[0] // 6
    adjoint, surfaces = station_part(residuals, station_cell, station_pairs, velocity.shape[1], velocity.shape[2], step_count)
    for window_step in range(step_count):
        strain_now = forward_strain[6 * window_step : 6 * window_step + 6]
        velocity, stress, lame_accum, shear_accum = advance(
            velocity, stress, lame_first, shear_modulus, buoyancy, strain_now, surfaces[window_step], lame_accum, shear_accum
        )
    return (velocity, stress, lame_accum, shear_accum, adjoint)


def solution(mesh):
    return jax.shard_map(
        shards,
        mesh=mesh,
        in_specs=(
            P(None, "gx", "gy", None),
            P(None, "gx", "gy", None),
            P("gx", "gy", None),
            P("gx", "gy", None),
            P("gx", "gy", None),
            P(None, "gx", "gy", None),
            P("gx", "gy", None),
            P("gx", "gy", None),
            P(("gx", "gy"), None),
            P(("gx", "gy")),
            P(),
        ),
        out_specs=(
            P(None, "gx", "gy", None),
            P(None, "gx", "gy", None),
            P("gx", "gy", None),
            P("gx", "gy", None),
            P(("gx", "gy"), None),
        ),
        check_vma=False,
    )
```

```python
import functools

import jax
import jax.numpy as jnp
from jax import lax
from jax.sharding import PartitionSpec as P
from jax.experimental import pallas as pl
from jax.experimental.pallas import tpu as pltpu

near_weight = 9.0 / 8.0
far_weight = -1.0 / 24.0
time_step = 0.25
epsilon = 1e-06


def shifted(padded, start, length, axis):
    return lax.slice_in_dim(padded, start, start + length, axis=axis)


def backward_diff(padded, length, axis):
    return near_weight * (
        shifted(padded, 2, length, axis) - shifted(padded, 1, length, axis)
    ) + far_weight * (shifted(padded, 3, length, axis) - shifted(padded, 0, length, axis))


def forward_diff(padded, length, axis):
    return near_weight * (
        shifted(padded, 3, length, axis) - shifted(padded, 2, length, axis)
    ) + far_weight * (shifted(padded, 4, length, axis) - shifted(padded, 1, length, axis))


def halo_pad(block, axis, dim, width=2):
    count = lax.axis_size(axis)
    forward = [(i, i + 1) for i in range(count - 1)]
    backward = [(i + 1, i) for i in range(count - 1)]
    size = block.shape[dim]
    low = lax.ppermute(lax.slice_in_dim(block, size - width, size, axis=dim), axis, forward)
    high = lax.ppermute(lax.slice_in_dim(block, 0, width, axis=dim), axis, backward)
    return jnp.concatenate([low, block, high], axis=dim)


def z_pad(block):
    pads = [(0, 0)] * (block.ndim - 1) + [(2, 2)]
    return jnp.pad(block, pads)


def exchange(block):
    wide_x = halo_pad(block[0], "gx", 1)
    wide_y = halo_pad(block[1], "gy", 2)
    return wide_x, wide_y


def advance(velocity, stress, lame_first, shear_modulus, buoyancy, strain_now, surface, lame_kernel, shear_kernel):
    nx = velocity.shape[1]
    ny = velocity.shape[2]
    nz = velocity.shape[3]
    sx, sy = exchange((jnp.stack([stress[0], stress[3], stress[4]]), jnp.stack([stress[3], stress[1], stress[5]])))
    sz = z_pad(jnp.stack([stress[4], stress[5], stress[2]]))
    force_first = forward_diff(sx[0], nx, 0) + backward_diff(sy[0], ny, 1) + backward_diff(sz[0], nz, 2)
    force_second = backward_diff(sx[1], nx, 0) + forward_diff(sy[1], ny, 1) + backward_diff(sz[1], nz, 2)
    force_third = backward_diff(sx[2], nx, 0) + backward_diff(sy[2], ny, 1) + forward_diff(sz[2], nz, 2)
    force_third = force_third.at[:, :, 0].add(surface)
    moved = velocity + time_step * buoyancy[None] * jnp.stack([force_first, force_second, force_third])
    mx, my = exchange((moved, moved))
    mz = z_pad(moved)
    rate_first = backward_diff(mx[0], nx, 0)
    rate_second = backward_diff(my[1], ny, 1)
    rate_third = backward_diff(mz[2], nz, 2)
    shear_one = forward_diff(my[0], ny, 1) + forward_diff(mx[1], nx, 0)
    shear_two = forward_diff(mz[0], nz, 2) + forward_diff(mx[2], nx, 0)
    shear_three = forward_diff(mz[1], nz, 2) + forward_diff(my[2], ny, 1)
    dilation = rate_first + rate_second + rate_third
    grown = stress + time_step * jnp.stack(
        [
            lame_first * dilation + 2.0 * shear_modulus * rate_first,
            lame_first * dilation + 2.0 * shear_modulus * rate_second,
            lame_first * dilation + 2.0 * shear_modulus * rate_third,
            shear_modulus * shear_one,
            shear_modulus * shear_two,
            shear_modulus * shear_three,
        ]
    )
    strain_vals = strain_now.astype(jnp.float32)
    lame_kernel = lame_kernel + time_step * (strain_vals[0] + strain_vals[1] + strain_vals[2]) * dilation
    shear_kernel = shear_kernel + 2.0 * time_step * (
        strain_vals[0] * rate_first
        + strain_vals[1] * rate_second
        + strain_vals[2] * rate_third
        + strain_vals[3] * shear_one
        + strain_vals[4] * shear_two
        + strain_vals[5] * shear_three
    )
    return (moved, grown, lame_kernel, shear_kernel)


def pair_kernel(block, samples, station_ref, table_ref, other_ref, out_ref, acc_ref, toward_ref, mine_ref):
    step = pl.program_id(0)

    @pl.when(step == 0)
    def _():
        acc_ref[...] = jnp.zeros_like(acc_ref)

    def pick(i, carry):
        mine_ref[i] = table_ref[station_ref[step * block + i]]
        return carry

    lax.fori_loop(0, block, pick, 0)
    mine_vals = mine_ref[...].astype(jnp.float32)
    other_vals = other_ref[...].astype(jnp.float32)
    mine_sq = jnp.sum(jnp.sum(mine_vals * mine_vals, axis=1, keepdims=True), axis=2, keepdims=True)
    other_sq = jnp.sum(jnp.sum(other_vals * other_vals, axis=1, keepdims=True), axis=2, keepdims=True)
    cross = jnp.sum(jnp.sum(mine_vals * other_vals, axis=1, keepdims=True), axis=2, keepdims=True)
    mine_norm = jnp.sqrt(mine_sq / samples + epsilon)
    other_norm = jnp.sqrt(other_sq / samples + epsilon)
    corr = (cross / samples) / (mine_norm * other_norm)
    other_scale = 1.0 / other_norm
    mine_scale = corr / mine_norm
    toward = other_vals * other_scale - mine_scale * mine_vals
    toward_ref[...] = toward.astype(jnp.bfloat16).astype(jnp.float32)

    ways = acc_ref.shape[0]

    def add_some(i, carry):
        for way in range(ways):
            slot = i * ways + way
            target = station_ref[step * block + slot]
            acc_ref[way, target] = acc_ref[way, target] + toward_ref[slot]
        return carry

    lax.fori_loop(0, block // ways, add_some, 0)

    @pl.when(step == pl.num_programs(0) - 1)
    def _():
        stations = out_ref.shape[0]
        total = acc_ref[0, :stations]
        for way in range(1, ways):
            total = total + acc_ref[way, :stations]
        out_ref[...] = total


def pair_sums(targets, table, other, stations):
    slots, rows, lanes = other.shape
    block = 64
    samples = rows * lanes
    spec = pl.BlockSpec((block, rows, lanes), lambda g, t: (g, 0, 0))
    return pl.pallas_call(
        functools.partial(pair_kernel, block, float(samples)),
        grid_spec=pltpu.PrefetchScalarGridSpec(
            num_scalar_prefetch=1,
            grid=(slots // block,),
            in_specs=[pl.BlockSpec(table.shape, lambda g, t: (0, 0, 0)), spec],
            out_specs=pl.BlockSpec((stations, rows, lanes), lambda g, t: (0, 0, 0)),
            scratch_shapes=[
                pltpu.VMEM((4, stations + 1, rows, lanes), jnp.float32),
                pltpu.VMEM((block, rows, lanes), jnp.float32),
                pltpu.VMEM((block, rows, lanes), table.dtype),
            ],
        ),
        out_shape=jax.ShapeDtypeStruct((stations, rows, lanes), jnp.float32),
        compiler_params=pltpu.CompilerParams(dimension_semantics=("arbitrary",)),
        cost_estimate=pl.CostEstimate(flops=20 * slots * samples, transcendentals=0, bytes_accessed=2 * slots * samples),
    )(targets, table, other)


def station_part(residuals, station_cell, station_pairs, cells_first, cells_second, step_count):
    stations_here = residuals.shape[0]
    samples = residuals.shape[1]
    devices = lax.axis_size(("gx", "gy"))
    pair_rows = station_pairs.shape[0] // devices
    me = lax.axis_index(("gx", "gy"))
    own = lax.dynamic_slice_in_dim(station_pairs, me * pair_rows, pair_rows, 0)
    first_local = own[:, 0] - me * stations_here
    dest = own[:, 1] // stations_here
    order = jnp.arange(pair_rows)
    same = (dest[:, None] == dest[None, :]) & (order[None, :] < order[:, None])
    rank = jnp.sum(same.astype(jnp.int32), axis=1)
    device_ids = jnp.arange(devices)
    pick_own = (dest[None, :, None] == device_ids[:, None, None]) & (rank[None, :, None] == jnp.arange(2)[None, None, :])
    own_station = jnp.sum(jnp.where(pick_own, first_local[None, :, None] + 1, 0), axis=1) - 1
    blocks = station_pairs.reshape(devices, pair_rows, 2)
    hit = (blocks[:, :, 1] // stations_here == me).astype(jnp.int32)
    before = jnp.cumsum(hit, axis=1) - hit
    pick_in = (hit[:, :, None] > 0) & (before[:, :, None] == jnp.arange(2)[None, None, :])
    in_station = jnp.sum(jnp.where(pick_in, (blocks[:, :, 1] % stations_here)[:, :, None] + 1, 0), axis=1) - 1
    slot_station = jnp.concatenate([own_station, in_station], axis=1)
    lanes = 128
    rows = residuals.reshape(stations_here, samples // lanes, lanes)
    padded_rows = jnp.concatenate([rows, jnp.zeros((1,) + rows.shape[1:], rows.dtype)], axis=0)
    send = padded_rows[jnp.where(slot_station >= 0, slot_station, stations_here)]
    recv = lax.all_to_all(send, ("gx", "gy"), split_axis=0, concat_axis=0, tiled=True)
    mine_station = jnp.concatenate([slot_station[:, 2:4], slot_station[:, 0:2]], axis=1)
    slots = devices * 4
    targets = jnp.where(mine_station >= 0, mine_station, stations_here).reshape(slots)
    adjoint3 = pair_sums(
        targets, padded_rows, recv.reshape(slots, samples // lanes, lanes), stations_here
    )
    adjoint = adjoint3.reshape(stations_here, samples)
    last = adjoint3[:, samples // lanes - 1, lanes - step_count :]
    tail = last
    cells_hit = (station_cell[:, None] == jnp.arange(cells_first * cells_second)[None, :]).astype(jnp.float32)
    surfaces = jnp.stack(
        [
            jnp.sum(cells_hit * tail[:, step_count - 1 - window_step][:, None], axis=0).reshape(cells_first, cells_second)
            for window_step in range(step_count)
        ]
    )
    return adjoint, surfaces


def shards(velocity, stress, lame_first, shear_modulus, buoyancy, forward_strain, lame_accum, shear_accum, residuals, station_cell, station_pairs):
    step_count = forward_strain.shape[0] // 6
    adjoint, surfaces = station_part(residuals, station_cell, station_pairs, velocity.shape[1], velocity.shape[2], step_count)
    for window_step in range(step_count):
        strain_now = forward_strain[6 * window_step : 6 * window_step + 6]
        velocity, stress, lame_accum, shear_accum = advance(
            velocity, stress, lame_first, shear_modulus, buoyancy, strain_now, surfaces[window_step], lame_accum, shear_accum
        )
    return (velocity, stress, lame_accum, shear_accum, adjoint)


def solution(mesh):
    return jax.shard_map(
        shards,
        mesh=mesh,
        in_specs=(
            P(None, "gx", "gy", None),
            P(None, "gx", "gy", None),
            P("gx", "gy", None),
            P("gx", "gy", None),
            P("gx", "gy", None),
            P(None, "gx", "gy", None),
            P("gx", "gy", None),
            P("gx", "gy", None),
            P(("gx", "gy"), None),
            P(("gx", "gy")),
            P(),
        ),
        out_specs=(
            P(None, "gx", "gy", None),
            P(None, "gx", "gy", None),
            P("gx", "gy", None),
            P("gx", "gy", None),
            P(("gx", "gy"), None),
        ),
        check_vma=False,
    )
```

```python
import functools

import jax
import jax.numpy as jnp
from jax import lax
from jax.sharding import PartitionSpec as P
from jax.experimental import pallas as pl
from jax.experimental.pallas import tpu as pltpu

near_weight = 9.0 / 8.0
far_weight = -1.0 / 24.0
time_step = 0.25
epsilon = 1e-06


def shifted(padded, start, length, axis):
    return lax.slice_in_dim(padded, start, start + length, axis=axis)


def backward_diff(padded, length, axis):
    return near_weight * (
        shifted(padded, 2, length, axis) - shifted(padded, 1, length, axis)
    ) + far_weight * (shifted(padded, 3, length, axis) - shifted(padded, 0, length, axis))


def forward_diff(padded, length, axis):
    return near_weight * (
        shifted(padded, 3, length, axis) - shifted(padded, 2, length, axis)
    ) + far_weight * (shifted(padded, 4, length, axis) - shifted(padded, 1, length, axis))


def halo_pad(block, axis, dim, width=2):
    count = lax.axis_size(axis)
    forward = [(i, i + 1) for i in range(count - 1)]
    backward = [(i + 1, i) for i in range(count - 1)]
    size = block.shape[dim]
    low = lax.ppermute(lax.slice_in_dim(block, size - width, size, axis=dim), axis, forward)
    high = lax.ppermute(lax.slice_in_dim(block, 0, width, axis=dim), axis, backward)
    return jnp.concatenate([low, block, high], axis=dim)


def z_pad(block):
    pads = [(0, 0)] * (block.ndim - 1) + [(2, 2)]
    return jnp.pad(block, pads)


def exchange(block):
    wide_x = halo_pad(block[0], "gx", 1)
    wide_y = halo_pad(block[1], "gy", 2)
    return wide_x, wide_y


def advance(velocity, stress, lame_first, shear_modulus, buoyancy, strain_now, surface, lame_kernel, shear_kernel):
    nx = velocity.shape[1]
    ny = velocity.shape[2]
    nz = velocity.shape[3]
    sx, sy = exchange((jnp.stack([stress[0], stress[3], stress[4]]), jnp.stack([stress[3], stress[1], stress[5]])))
    sz = z_pad(jnp.stack([stress[4], stress[5], stress[2]]))
    force_first = forward_diff(sx[0], nx, 0) + backward_diff(sy[0], ny, 1) + backward_diff(sz[0], nz, 2)
    force_second = backward_diff(sx[1], nx, 0) + forward_diff(sy[1], ny, 1) + backward_diff(sz[1], nz, 2)
    force_third = backward_diff(sx[2], nx, 0) + backward_diff(sy[2], ny, 1) + forward_diff(sz[2], nz, 2)
    force_third = force_third.at[:, :, 0].add(surface)
    moved = velocity + time_step * buoyancy[None] * jnp.stack([force_first, force_second, force_third])
    mx, my = exchange((moved, moved))
    mz = z_pad(moved)
    rate_first = backward_diff(mx[0], nx, 0)
    rate_second = backward_diff(my[1], ny, 1)
    rate_third = backward_diff(mz[2], nz, 2)
    shear_one = forward_diff(my[0], ny, 1) + forward_diff(mx[1], nx, 0)
    shear_two = forward_diff(mz[0], nz, 2) + forward_diff(mx[2], nx, 0)
    shear_three = forward_diff(mz[1], nz, 2) + forward_diff(my[2], ny, 1)
    dilation = rate_first + rate_second + rate_third
    grown = stress + time_step * jnp.stack(
        [
            lame_first * dilation + 2.0 * shear_modulus * rate_first,
            lame_first * dilation + 2.0 * shear_modulus * rate_second,
            lame_first * dilation + 2.0 * shear_modulus * rate_third,
            shear_modulus * shear_one,
            shear_modulus * shear_two,
            shear_modulus * shear_three,
        ]
    )
    strain_vals = strain_now.astype(jnp.float32)
    lame_kernel = lame_kernel + time_step * (strain_vals[0] + strain_vals[1] + strain_vals[2]) * dilation
    shear_kernel = shear_kernel + 2.0 * time_step * (
        strain_vals[0] * rate_first
        + strain_vals[1] * rate_second
        + strain_vals[2] * rate_third
        + strain_vals[3] * shear_one
        + strain_vals[4] * shear_two
        + strain_vals[5] * shear_three
    )
    return (moved, grown, lame_kernel, shear_kernel)


def pair_kernel(block, samples, station_ref, mine_ref, other_ref, out_ref, acc_ref, toward_ref):
    step = pl.program_id(0)

    @pl.when(step == 0)
    def _():
        acc_ref[...] = jnp.zeros_like(acc_ref)

    mine_vals = mine_ref[...].astype(jnp.float32)
    other_vals = other_ref[...].astype(jnp.float32)
    mine_sq = jnp.sum(jnp.sum(mine_vals * mine_vals, axis=1, keepdims=True), axis=2, keepdims=True)
    other_sq = jnp.sum(jnp.sum(other_vals * other_vals, axis=1, keepdims=True), axis=2, keepdims=True)
    cross = jnp.sum(jnp.sum(mine_vals * other_vals, axis=1, keepdims=True), axis=2, keepdims=True)
    mine_norm = jnp.sqrt(mine_sq / samples + epsilon)
    other_norm = jnp.sqrt(other_sq / samples + epsilon)
    corr = (cross / samples) / (mine_norm * other_norm)
    other_scale = 1.0 / other_norm
    mine_scale = corr / mine_norm
    toward = other_vals * other_scale - mine_scale * mine_vals
    toward_ref[...] = toward.astype(jnp.bfloat16).astype(jnp.float32)

    ways = acc_ref.shape[0]

    def add_some(i, carry):
        for way in range(ways):
            slot = i * ways + way
            target = station_ref[step * block + slot]
            acc_ref[way, target] = acc_ref[way, target] + toward_ref[slot]
        return carry

    lax.fori_loop(0, block // ways, add_some, 0)

    @pl.when(step == pl.num_programs(0) - 1)
    def _():
        stations = out_ref.shape[0]
        total = acc_ref[0, :stations]
        for way in range(1, ways):
            total = total + acc_ref[way, :stations]
        out_ref[...] = total


def pair_sums(targets, mine, other, stations):
    slots, rows, lanes = mine.shape
    block = 128
    samples = rows * lanes
    spec = pl.BlockSpec((block, rows, lanes), lambda g, t: (g, 0, 0))
    return pl.pallas_call(
        functools.partial(pair_kernel, block, float(samples)),
        grid_spec=pltpu.PrefetchScalarGridSpec(
            num_scalar_prefetch=1,
            grid=(slots // block,),
            in_specs=[spec, spec],
            out_specs=pl.BlockSpec((stations, rows, lanes), lambda g, t: (0, 0, 0)),
            scratch_shapes=[
                pltpu.VMEM((4, stations + 1, rows, lanes), jnp.float32),
                pltpu.VMEM((block, rows, lanes), jnp.float32),
            ],
        ),
        out_shape=jax.ShapeDtypeStruct((stations, rows, lanes), jnp.float32),
        compiler_params=pltpu.CompilerParams(dimension_semantics=("arbitrary",)),
        cost_estimate=pl.CostEstimate(flops=20 * slots * samples, transcendentals=0, bytes_accessed=4 * slots * samples),
    )(targets, mine, other)


def station_part(residuals, station_cell, station_pairs, cells_first, cells_second, step_count):
    stations_here = residuals.shape[0]
    samples = residuals.shape[1]
    devices = lax.axis_size(("gx", "gy"))
    pair_rows = station_pairs.shape[0] // devices
    me = lax.axis_index(("gx", "gy"))
    own = lax.dynamic_slice_in_dim(station_pairs, me * pair_rows, pair_rows, 0)
    first_local = own[:, 0] - me * stations_here
    dest = own[:, 1] // stations_here
    order = jnp.arange(pair_rows)
    same = (dest[:, None] == dest[None, :]) & (order[None, :] < order[:, None])
    rank = jnp.sum(same.astype(jnp.int32), axis=1)
    device_ids = jnp.arange(devices)
    pick_own = (dest[None, :, None] == device_ids[:, None, None]) & (rank[None, :, None] == jnp.arange(2)[None, None, :])
    own_station = jnp.sum(jnp.where(pick_own, first_local[None, :, None] + 1, 0), axis=1) - 1
    blocks = station_pairs.reshape(devices, pair_rows, 2)
    hit = (blocks[:, :, 1] // stations_here == me).astype(jnp.int32)
    before = jnp.cumsum(hit, axis=1) - hit
    pick_in = (hit[:, :, None] > 0) & (before[:, :, None] == jnp.arange(2)[None, None, :])
    in_station = jnp.sum(jnp.where(pick_in, (blocks[:, :, 1] % stations_here)[:, :, None] + 1, 0), axis=1) - 1
    slot_station = jnp.concatenate([own_station, in_station], axis=1)
    lanes = 128
    rows = residuals.reshape(stations_here, samples // lanes, lanes)
    padded_rows = jnp.concatenate([rows, jnp.zeros((1,) + rows.shape[1:], rows.dtype)], axis=0)
    send = padded_rows[jnp.where(slot_station >= 0, slot_station, stations_here)]
    recv = lax.all_to_all(send, ("gx", "gy"), split_axis=0, concat_axis=0, tiled=True)
    mine_station = jnp.concatenate([slot_station[:, 2:4], slot_station[:, 0:2]], axis=1)
    mine = padded_rows[jnp.where(mine_station >= 0, mine_station, stations_here)]
    slots = devices * 4
    targets = jnp.where(mine_station >= 0, mine_station, stations_here).reshape(slots)
    adjoint3 = pair_sums(
        targets, mine.reshape(slots, samples // lanes, lanes), recv.reshape(slots, samples // lanes, lanes), stations_here
    )
    adjoint = adjoint3.reshape(stations_here, samples)
    last = adjoint3[:, samples // lanes - 1, lanes - step_count :]
    tail = last
    cells_hit = (station_cell[:, None] == jnp.arange(cells_first * cells_second)[None, :]).astype(jnp.float32)
    surfaces = jnp.stack(
        [
            jnp.sum(cells_hit * tail[:, step_count - 1 - window_step][:, None], axis=0).reshape(cells_first, cells_second)
            for window_step in range(step_count)
        ]
    )
    return adjoint, surfaces


def shards(velocity, stress, lame_first, shear_modulus, buoyancy, forward_strain, lame_accum, shear_accum, residuals, station_cell, station_pairs):
    step_count = forward_strain.shape[0] // 6
    adjoint, surfaces = station_part(residuals, station_cell, station_pairs, velocity.shape[1], velocity.shape[2], step_count)
    for window_step in range(step_count):
        strain_now = forward_strain[6 * window_step : 6 * window_step + 6]
        velocity, stress, lame_accum, shear_accum = advance(
            velocity, stress, lame_first, shear_modulus, buoyancy, strain_now, surfaces[window_step], lame_accum, shear_accum
        )
    return (velocity, stress, lame_accum, shear_accum, adjoint)


def solution(mesh):
    return jax.shard_map(
        shards,
        mesh=mesh,
        in_specs=(
            P(None, "gx", "gy", None),
            P(None, "gx", "gy", None),
            P("gx", "gy", None),
            P("gx", "gy", None),
            P("gx", "gy", None),
            P(None, "gx", "gy", None),
            P("gx", "gy", None),
            P("gx", "gy", None),
            P(("gx", "gy"), None),
            P(("gx", "gy")),
            P(),
        ),
        out_specs=(
            P(None, "gx", "gy", None),
            P(None, "gx", "gy", None),
            P("gx", "gy", None),
            P("gx", "gy", None),
            P(("gx", "gy"), None),
        ),
        check_vma=False,
    )
```

```python
import functools

import jax
import jax.numpy as jnp
from jax import lax
from jax.sharding import PartitionSpec as P
from jax.experimental import pallas as pl
from jax.experimental.pallas import tpu as pltpu

near_weight = 9.0 / 8.0
far_weight = -1.0 / 24.0
time_step = 0.25
epsilon = 1e-06


def shifted(padded, start, length, axis):
    return lax.slice_in_dim(padded, start, start + length, axis=axis)


def backward_diff(padded, length, axis):
    return near_weight * (
        shifted(padded, 2, length, axis) - shifted(padded, 1, length, axis)
    ) + far_weight * (shifted(padded, 3, length, axis) - shifted(padded, 0, length, axis))


def forward_diff(padded, length, axis):
    return near_weight * (
        shifted(padded, 3, length, axis) - shifted(padded, 2, length, axis)
    ) + far_weight * (shifted(padded, 4, length, axis) - shifted(padded, 1, length, axis))


def halo_pad(block, axis, dim, width=2):
    count = lax.axis_size(axis)
    forward = [(i, i + 1) for i in range(count - 1)]
    backward = [(i + 1, i) for i in range(count - 1)]
    size = block.shape[dim]
    low = lax.ppermute(lax.slice_in_dim(block, size - width, size, axis=dim), axis, forward)
    high = lax.ppermute(lax.slice_in_dim(block, 0, width, axis=dim), axis, backward)
    return jnp.concatenate([low, block, high], axis=dim)


def z_pad(block):
    pads = [(0, 0)] * (block.ndim - 1) + [(2, 2)]
    return jnp.pad(block, pads)


def exchange(block):
    wide_x = halo_pad(block[0], "gx", 1)
    wide_y = halo_pad(block[1], "gy", 2)
    return wide_x, wide_y


def advance(velocity, stress, lame_first, shear_modulus, buoyancy, strain_now, surface, lame_kernel, shear_kernel):
    nx = velocity.shape[1]
    ny = velocity.shape[2]
    nz = velocity.shape[3]
    sx, sy = exchange((jnp.stack([stress[0], stress[3], stress[4]]), jnp.stack([stress[3], stress[1], stress[5]])))
    sz = z_pad(jnp.stack([stress[4], stress[5], stress[2]]))
    force_first = forward_diff(sx[0], nx, 0) + backward_diff(sy[0], ny, 1) + backward_diff(sz[0], nz, 2)
    force_second = backward_diff(sx[1], nx, 0) + forward_diff(sy[1], ny, 1) + backward_diff(sz[1], nz, 2)
    force_third = backward_diff(sx[2], nx, 0) + backward_diff(sy[2], ny, 1) + forward_diff(sz[2], nz, 2)
    force_third = force_third.at[:, :, 0].add(surface)
    moved = velocity + time_step * buoyancy[None] * jnp.stack([force_first, force_second, force_third])
    mx, my = exchange((moved, moved))
    mz = z_pad(moved)
    rate_first = backward_diff(mx[0], nx, 0)
    rate_second = backward_diff(my[1], ny, 1)
    rate_third = backward_diff(mz[2], nz, 2)
    shear_one = forward_diff(my[0], ny, 1) + forward_diff(mx[1], nx, 0)
    shear_two = forward_diff(mz[0], nz, 2) + forward_diff(mx[2], nx, 0)
    shear_three = forward_diff(mz[1], nz, 2) + forward_diff(my[2], ny, 1)
    dilation = rate_first + rate_second + rate_third
    grown = stress + time_step * jnp.stack(
        [
            lame_first * dilation + 2.0 * shear_modulus * rate_first,
            lame_first * dilation + 2.0 * shear_modulus * rate_second,
            lame_first * dilation + 2.0 * shear_modulus * rate_third,
            shear_modulus * shear_one,
            shear_modulus * shear_two,
            shear_modulus * shear_three,
        ]
    )
    strain_vals = strain_now.astype(jnp.float32)
    lame_kernel = lame_kernel + time_step * (strain_vals[0] + strain_vals[1] + strain_vals[2]) * dilation
    shear_kernel = shear_kernel + 2.0 * time_step * (
        strain_vals[0] * rate_first
        + strain_vals[1] * rate_second
        + strain_vals[2] * rate_third
        + strain_vals[3] * shear_one
        + strain_vals[4] * shear_two
        + strain_vals[5] * shear_three
    )
    return (moved, grown, lame_kernel, shear_kernel)


def pair_kernel(block, samples, station_ref, mine_ref, other_ref, out_ref, last_ref, acc_ref, toward_ref):
    step = pl.program_id(0)

    @pl.when(step == 0)
    def _():
        acc_ref[...] = jnp.zeros_like(acc_ref)

    mine_vals = mine_ref[...].astype(jnp.float32)
    other_vals = other_ref[...].astype(jnp.float32)
    mine_sq = jnp.sum(jnp.sum(mine_vals * mine_vals, axis=1, keepdims=True), axis=2, keepdims=True)
    other_sq = jnp.sum(jnp.sum(other_vals * other_vals, axis=1, keepdims=True), axis=2, keepdims=True)
    cross = jnp.sum(jnp.sum(mine_vals * other_vals, axis=1, keepdims=True), axis=2, keepdims=True)
    mine_norm = jnp.sqrt(mine_sq / samples + epsilon)
    other_norm = jnp.sqrt(other_sq / samples + epsilon)
    corr = (cross / samples) / (mine_norm * other_norm)
    toward = other_vals / other_norm - corr * (mine_vals / mine_norm)
    toward_ref[...] = toward.astype(jnp.bfloat16).astype(jnp.float32)

    ways = acc_ref.shape[0]

    def add_some(i, carry):
        for way in range(ways):
            slot = i * ways + way
            target = station_ref[step * block + slot]
            acc_ref[way, target] = acc_ref[way, target] + toward_ref[slot]
        return carry

    lax.fori_loop(0, block // ways, add_some, 0)

    @pl.when(step == pl.num_programs(0) - 1)
    def _():
        stations = out_ref.shape[0]
        total = acc_ref[0, :stations]
        for way in range(1, ways):
            total = total + acc_ref[way, :stations]
        out_ref[...] = total
        last_ref[...] = total[:, total.shape[1] - 1 :, :]


def pair_sums(targets, mine, other, stations):
    slots, rows, lanes = mine.shape
    block = 64
    samples = rows * lanes
    spec = pl.BlockSpec((block, rows, lanes), lambda g, t: (g, 0, 0))
    return pl.pallas_call(
        functools.partial(pair_kernel, block, float(samples)),
        grid_spec=pltpu.PrefetchScalarGridSpec(
            num_scalar_prefetch=1,
            grid=(slots // block,),
            in_specs=[spec, spec],
            out_specs=[
                pl.BlockSpec((stations, rows, lanes), lambda g, t: (0, 0, 0)),
                pl.BlockSpec((stations, 1, lanes), lambda g, t: (0, 0, 0)),
            ],
            scratch_shapes=[
                pltpu.VMEM((4, stations + 1, rows, lanes), jnp.float32),
                pltpu.VMEM((block, rows, lanes), jnp.float32),
            ],
        ),
        out_shape=[
            jax.ShapeDtypeStruct((stations, rows, lanes), jnp.float32),
            jax.ShapeDtypeStruct((stations, 1, lanes), jnp.float32),
        ],
        compiler_params=pltpu.CompilerParams(dimension_semantics=("arbitrary",)),
        cost_estimate=pl.CostEstimate(flops=20 * slots * samples, transcendentals=0, bytes_accessed=4 * slots * samples),
    )(targets, mine, other)


def station_part(residuals, station_cell, station_pairs, cells_first, cells_second, step_count):
    stations_here = residuals.shape[0]
    samples = residuals.shape[1]
    devices = lax.axis_size(("gx", "gy"))
    pair_rows = station_pairs.shape[0] // devices
    me = lax.axis_index(("gx", "gy"))
    own = lax.dynamic_slice_in_dim(station_pairs, me * pair_rows, pair_rows, 0)
    first_local = own[:, 0] - me * stations_here
    dest = own[:, 1] // stations_here
    order = jnp.arange(pair_rows)
    same = (dest[:, None] == dest[None, :]) & (order[None, :] < order[:, None])
    rank = jnp.sum(same.astype(jnp.int32), axis=1)
    device_ids = jnp.arange(devices)
    pick_own = (dest[None, :, None] == device_ids[:, None, None]) & (rank[None, :, None] == jnp.arange(2)[None, None, :])
    own_station = jnp.sum(jnp.where(pick_own, first_local[None, :, None] + 1, 0), axis=1) - 1
    blocks = station_pairs.reshape(devices, pair_rows, 2)
    hit = (blocks[:, :, 1] // stations_here == me).astype(jnp.int32)
    before = jnp.cumsum(hit, axis=1) - hit
    pick_in = (hit[:, :, None] > 0) & (before[:, :, None] == jnp.arange(2)[None, None, :])
    in_station = jnp.sum(jnp.where(pick_in, (blocks[:, :, 1] % stations_here)[:, :, None] + 1, 0), axis=1) - 1
    slot_station = jnp.concatenate([own_station, in_station], axis=1)
    lanes = 128
    rows = residuals.reshape(stations_here, samples // lanes, lanes)
    padded_rows = jnp.concatenate([rows, jnp.zeros((1,) + rows.shape[1:], rows.dtype)], axis=0)
    send = padded_rows[jnp.where(slot_station >= 0, slot_station, stations_here)]
    recv = lax.all_to_all(send, ("gx", "gy"), split_axis=0, concat_axis=0, tiled=True)
    mine_station = jnp.concatenate([slot_station[:, 2:4], slot_station[:, 0:2]], axis=1)
    mine = padded_rows[jnp.where(mine_station >= 0, mine_station, stations_here)]
    slots = devices * 4
    targets = jnp.where(mine_station >= 0, mine_station, stations_here).reshape(slots)
    adjoint3, last_rows = pair_sums(
        targets, mine.reshape(slots, samples // lanes, lanes), recv.reshape(slots, samples // lanes, lanes), stations_here
    )
    adjoint = adjoint3.reshape(stations_here, samples)
    last = last_rows[:, 0, lanes - step_count :]
    tail = last
    cells_hit = (station_cell[:, None] == jnp.arange(cells_first * cells_second)[None, :]).astype(jnp.float32)
    surfaces = jnp.stack(
        [
            jnp.sum(cells_hit * tail[:, step_count - 1 - window_step][:, None], axis=0).reshape(cells_first, cells_second)
            for window_step in range(step_count)
        ]
    )
    return adjoint, surfaces


def shards(velocity, stress, lame_first, shear_modulus, buoyancy, forward_strain, lame_accum, shear_accum, residuals, station_cell, station_pairs):
    step_count = forward_strain.shape[0] // 6
    adjoint, surfaces = station_part(residuals, station_cell, station_pairs, velocity.shape[1], velocity.shape[2], step_count)
    for window_step in range(step_count):
        strain_now = forward_strain[6 * window_step : 6 * window_step + 6]
        velocity, stress, lame_accum, shear_accum = advance(
            velocity, stress, lame_first, shear_modulus, buoyancy, strain_now, surfaces[window_step], lame_accum, shear_accum
        )
    return (velocity, stress, lame_accum, shear_accum, adjoint)


def solution(mesh):
    return jax.shard_map(
        shards,
        mesh=mesh,
        in_specs=(
            P(None, "gx", "gy", None),
            P(None, "gx", "gy", None),
            P("gx", "gy", None),
            P("gx", "gy", None),
            P("gx", "gy", None),
            P(None, "gx", "gy", None),
            P("gx", "gy", None),
            P("gx", "gy", None),
            P(("gx", "gy"), None),
            P(("gx", "gy")),
            P(),
        ),
        out_specs=(
            P(None, "gx", "gy", None),
            P(None, "gx", "gy", None),
            P("gx", "gy", None),
            P("gx", "gy", None),
            P(("gx", "gy"), None),
        ),
        check_vma=False,
    )
```

```python
import functools

import jax
import jax.numpy as jnp
from jax import lax
from jax.sharding import PartitionSpec as P
from jax.experimental import pallas as pl
from jax.experimental.pallas import tpu as pltpu

near_weight = 9.0 / 8.0
far_weight = -1.0 / 24.0
time_step = 0.25
epsilon = 1e-06


def shifted(padded, start, length, axis):
    return lax.slice_in_dim(padded, start, start + length, axis=axis)


def backward_diff(padded, length, axis):
    return near_weight * (
        shifted(padded, 2, length, axis) - shifted(padded, 1, length, axis)
    ) + far_weight * (shifted(padded, 3, length, axis) - shifted(padded, 0, length, axis))


def forward_diff(padded, length, axis):
    return near_weight * (
        shifted(padded, 3, length, axis) - shifted(padded, 2, length, axis)
    ) + far_weight * (shifted(padded, 4, length, axis) - shifted(padded, 1, length, axis))


def halo_pad(block, axis, dim, width=2):
    count = lax.axis_size(axis)
    forward = [(i, i + 1) for i in range(count - 1)]
    backward = [(i + 1, i) for i in range(count - 1)]
    size = block.shape[dim]
    low = lax.ppermute(lax.slice_in_dim(block, size - width, size, axis=dim), axis, forward)
    high = lax.ppermute(lax.slice_in_dim(block, 0, width, axis=dim), axis, backward)
    return jnp.concatenate([low, block, high], axis=dim)


def z_pad(block):
    pads = [(0, 0)] * (block.ndim - 1) + [(2, 2)]
    return jnp.pad(block, pads)


def exchange(block):
    wide_x = halo_pad(block[0], "gx", 1)
    wide_y = halo_pad(block[1], "gy", 2)
    return wide_x, wide_y


def advance(velocity, stress, lame_first, shear_modulus, buoyancy, strain_now, surface, lame_kernel, shear_kernel):
    nx = velocity.shape[1]
    ny = velocity.shape[2]
    nz = velocity.shape[3]
    sx, sy = exchange((jnp.stack([stress[0], stress[3], stress[4]]), jnp.stack([stress[3], stress[1], stress[5]])))
    sz = z_pad(jnp.stack([stress[4], stress[5], stress[2]]))
    force_first = forward_diff(sx[0], nx, 0) + backward_diff(sy[0], ny, 1) + backward_diff(sz[0], nz, 2)
    force_second = backward_diff(sx[1], nx, 0) + forward_diff(sy[1], ny, 1) + backward_diff(sz[1], nz, 2)
    force_third = backward_diff(sx[2], nx, 0) + backward_diff(sy[2], ny, 1) + forward_diff(sz[2], nz, 2)
    force_third = force_third.at[:, :, 0].add(surface)
    moved = velocity + time_step * buoyancy[None] * jnp.stack([force_first, force_second, force_third])
    mx, my = exchange((moved, moved))
    mz = z_pad(moved)
    rate_first = backward_diff(mx[0], nx, 0)
    rate_second = backward_diff(my[1], ny, 1)
    rate_third = backward_diff(mz[2], nz, 2)
    shear_one = forward_diff(my[0], ny, 1) + forward_diff(mx[1], nx, 0)
    shear_two = forward_diff(mz[0], nz, 2) + forward_diff(mx[2], nx, 0)
    shear_three = forward_diff(mz[1], nz, 2) + forward_diff(my[2], ny, 1)
    dilation = rate_first + rate_second + rate_third
    grown = stress + time_step * jnp.stack(
        [
            lame_first * dilation + 2.0 * shear_modulus * rate_first,
            lame_first * dilation + 2.0 * shear_modulus * rate_second,
            lame_first * dilation + 2.0 * shear_modulus * rate_third,
            shear_modulus * shear_one,
            shear_modulus * shear_two,
            shear_modulus * shear_three,
        ]
    )
    strain_vals = strain_now.astype(jnp.float32)
    lame_kernel = lame_kernel + time_step * (strain_vals[0] + strain_vals[1] + strain_vals[2]) * dilation
    shear_kernel = shear_kernel + 2.0 * time_step * (
        strain_vals[0] * rate_first
        + strain_vals[1] * rate_second
        + strain_vals[2] * rate_third
        + strain_vals[3] * shear_one
        + strain_vals[4] * shear_two
        + strain_vals[5] * shear_three
    )
    return (moved, grown, lame_kernel, shear_kernel)


def pair_kernel(block, samples, station_ref, mine_ref, other_ref, mine_sq_ref, out_ref, acc_ref, toward_ref):
    step = pl.program_id(0)

    @pl.when(step == 0)
    def _():
        acc_ref[...] = jnp.zeros_like(acc_ref)

    mine_vals = mine_ref[...].astype(jnp.float32)
    other_vals = other_ref[...].astype(jnp.float32)
    mine_sq = mine_sq_ref[...][:, :, :1]
    other_sq = jnp.sum(jnp.sum(other_vals * other_vals, axis=1, keepdims=True), axis=2, keepdims=True)
    cross = jnp.sum(jnp.sum(mine_vals * other_vals, axis=1, keepdims=True), axis=2, keepdims=True)
    mine_norm = jnp.sqrt(mine_sq / samples + epsilon)
    other_norm = jnp.sqrt(other_sq / samples + epsilon)
    corr = (cross / samples) / (mine_norm * other_norm)
    toward = other_vals / other_norm - corr * (mine_vals / mine_norm)
    toward_ref[...] = toward.astype(jnp.bfloat16).astype(jnp.float32)

    ways = acc_ref.shape[0]

    def add_some(i, carry):
        for way in range(ways):
            slot = i * ways + way
            target = station_ref[step * block + slot]
            acc_ref[way, target] = acc_ref[way, target] + toward_ref[slot]
        return carry

    lax.fori_loop(0, block // ways, add_some, 0)

    @pl.when(step == pl.num_programs(0) - 1)
    def _():
        stations = out_ref.shape[0]
        total = acc_ref[0, :stations]
        for way in range(1, ways):
            total = total + acc_ref[way, :stations]
        out_ref[...] = total


def pair_sums(targets, mine, other, mine_sq, stations):
    slots, rows, lanes = mine.shape
    block = 64
    samples = rows * lanes
    spec = pl.BlockSpec((block, rows, lanes), lambda g, t: (g, 0, 0))
    return pl.pallas_call(
        functools.partial(pair_kernel, block, float(samples)),
        grid_spec=pltpu.PrefetchScalarGridSpec(
            num_scalar_prefetch=1,
            grid=(slots // block,),
            in_specs=[spec, spec, pl.BlockSpec((block, 1, lanes), lambda g, t: (g, 0, 0))],
            out_specs=pl.BlockSpec((stations, rows, lanes), lambda g, t: (0, 0, 0)),
            scratch_shapes=[
                pltpu.VMEM((4, stations + 1, rows, lanes), jnp.float32),
                pltpu.VMEM((block, rows, lanes), jnp.float32),
            ],
        ),
        out_shape=jax.ShapeDtypeStruct((stations, rows, lanes), jnp.float32),
        compiler_params=pltpu.CompilerParams(dimension_semantics=("arbitrary",)),
        cost_estimate=pl.CostEstimate(flops=20 * slots * samples, transcendentals=0, bytes_accessed=4 * slots * samples),
    )(targets, mine, other, mine_sq)


def station_part(residuals, station_cell, station_pairs, cells_first, cells_second, step_count):
    stations_here = residuals.shape[0]
    samples = residuals.shape[1]
    devices = lax.axis_size(("gx", "gy"))
    pair_rows = station_pairs.shape[0] // devices
    me = lax.axis_index(("gx", "gy"))
    own = lax.dynamic_slice_in_dim(station_pairs, me * pair_rows, pair_rows, 0)
    first_local = own[:, 0] - me * stations_here
    dest = own[:, 1] // stations_here
    order = jnp.arange(pair_rows)
    same = (dest[:, None] == dest[None, :]) & (order[None, :] < order[:, None])
    rank = jnp.sum(same.astype(jnp.int32), axis=1)
    device_ids = jnp.arange(devices)
    pick_own = (dest[None, :, None] == device_ids[:, None, None]) & (rank[None, :, None] == jnp.arange(2)[None, None, :])
    own_station = jnp.sum(jnp.where(pick_own, first_local[None, :, None] + 1, 0), axis=1) - 1
    blocks = station_pairs.reshape(devices, pair_rows, 2)
    hit = (blocks[:, :, 1] // stations_here == me).astype(jnp.int32)
    before = jnp.cumsum(hit, axis=1) - hit
    pick_in = (hit[:, :, None] > 0) & (before[:, :, None] == jnp.arange(2)[None, None, :])
    in_station = jnp.sum(jnp.where(pick_in, (blocks[:, :, 1] % stations_here)[:, :, None] + 1, 0), axis=1) - 1
    slot_station = jnp.concatenate([own_station, in_station], axis=1)
    lanes = 128
    rows = residuals.reshape(stations_here, samples // lanes, lanes)
    padded_rows = jnp.concatenate([rows, jnp.zeros((1,) + rows.shape[1:], rows.dtype)], axis=0)
    send = padded_rows[jnp.where(slot_station >= 0, slot_station, stations_here)]
    recv = lax.all_to_all(send, ("gx", "gy"), split_axis=0, concat_axis=0, tiled=True)
    mine_station = jnp.concatenate([slot_station[:, 2:4], slot_station[:, 0:2]], axis=1)
    mine = padded_rows[jnp.where(mine_station >= 0, mine_station, stations_here)]
    slots = devices * 4
    targets = jnp.where(mine_station >= 0, mine_station, stations_here).reshape(slots)
    row_vals = padded_rows.astype(jnp.float32)
    station_sq = jnp.sum(jnp.sum(row_vals * row_vals, axis=1), axis=1)
    slot_sq = jnp.broadcast_to(station_sq[targets][:, None, None], (slots, 1, lanes))
    adjoint3 = pair_sums(
        targets, mine.reshape(slots, samples // lanes, lanes), recv.reshape(slots, samples // lanes, lanes), slot_sq, stations_here
    )
    adjoint = adjoint3.reshape(stations_here, samples)
    last = adjoint3[:, samples // lanes - 1, lanes - step_count :]
    tail = last
    cells_hit = (station_cell[:, None] == jnp.arange(cells_first * cells_second)[None, :]).astype(jnp.float32)
    surfaces = jnp.stack(
        [
            jnp.sum(cells_hit * tail[:, step_count - 1 - window_step][:, None], axis=0).reshape(cells_first, cells_second)
            for window_step in range(step_count)
        ]
    )
    return adjoint, surfaces


def shards(velocity, stress, lame_first, shear_modulus, buoyancy, forward_strain, lame_accum, shear_accum, residuals, station_cell, station_pairs):
    step_count = forward_strain.shape[0] // 6
    adjoint, surfaces = station_part(residuals, station_cell, station_pairs, velocity.shape[1], velocity.shape[2], step_count)
    for window_step in range(step_count):
        strain_now = forward_strain[6 * window_step : 6 * window_step + 6]
        velocity, stress, lame_accum, shear_accum = advance(
            velocity, stress, lame_first, shear_modulus, buoyancy, strain_now, surfaces[window_step], lame_accum, shear_accum
        )
    return (velocity, stress, lame_accum, shear_accum, adjoint)


def solution(mesh):
    return jax.shard_map(
        shards,
        mesh=mesh,
        in_specs=(
            P(None, "gx", "gy", None),
            P(None, "gx", "gy", None),
            P("gx", "gy", None),
            P("gx", "gy", None),
            P("gx", "gy", None),
            P(None, "gx", "gy", None),
            P("gx", "gy", None),
            P("gx", "gy", None),
            P(("gx", "gy"), None),
            P(("gx", "gy")),
            P(),
        ),
        out_specs=(
            P(None, "gx", "gy", None),
            P(None, "gx", "gy", None),
            P("gx", "gy", None),
            P("gx", "gy", None),
            P(("gx", "gy"), None),
        ),
        check_vma=False,
    )
```

```python
import functools

import jax
import jax.numpy as jnp
from jax import lax
from jax.sharding import PartitionSpec as P
from jax.experimental import pallas as pl
from jax.experimental.pallas import tpu as pltpu

near_weight = 9.0 / 8.0
far_weight = -1.0 / 24.0
time_step = 0.25
epsilon = 1e-06


def shifted(padded, start, length, axis):
    return lax.slice_in_dim(padded, start, start + length, axis=axis)


def backward_diff(padded, length, axis):
    return near_weight * (
        shifted(padded, 2, length, axis) - shifted(padded, 1, length, axis)
    ) + far_weight * (shifted(padded, 3, length, axis) - shifted(padded, 0, length, axis))


def forward_diff(padded, length, axis):
    return near_weight * (
        shifted(padded, 3, length, axis) - shifted(padded, 2, length, axis)
    ) + far_weight * (shifted(padded, 4, length, axis) - shifted(padded, 1, length, axis))


def halo_pad(block, axis, dim, width=2):
    count = lax.axis_size(axis)
    forward = [(i, i + 1) for i in range(count - 1)]
    backward = [(i + 1, i) for i in range(count - 1)]
    size = block.shape[dim]
    low = lax.ppermute(lax.slice_in_dim(block, size - width, size, axis=dim), axis, forward)
    high = lax.ppermute(lax.slice_in_dim(block, 0, width, axis=dim), axis, backward)
    return jnp.concatenate([low, block, high], axis=dim)


def z_pad(block):
    pads = [(0, 0)] * (block.ndim - 1) + [(2, 2)]
    return jnp.pad(block, pads)


def exchange(block):
    wide_x = halo_pad(block[0], "gx", 1)
    wide_y = halo_pad(block[1], "gy", 2)
    return wide_x, wide_y


def advance(velocity, stress, lame_first, shear_modulus, buoyancy, strain_now, surface, lame_kernel, shear_kernel):
    nx = velocity.shape[1]
    ny = velocity.shape[2]
    nz = velocity.shape[3]
    sx, sy = exchange((jnp.stack([stress[0], stress[3], stress[4]]), jnp.stack([stress[3], stress[1], stress[5]])))
    sz = z_pad(jnp.stack([stress[4], stress[5], stress[2]]))
    force_first = forward_diff(sx[0], nx, 0) + backward_diff(sy[0], ny, 1) + backward_diff(sz[0], nz, 2)
    force_second = backward_diff(sx[1], nx, 0) + forward_diff(sy[1], ny, 1) + backward_diff(sz[1], nz, 2)
    force_third = backward_diff(sx[2], nx, 0) + backward_diff(sy[2], ny, 1) + forward_diff(sz[2], nz, 2)
    force_third = force_third.at[:, :, 0].add(surface)
    moved = velocity + time_step * buoyancy[None] * jnp.stack([force_first, force_second, force_third])
    mx, my = exchange((moved, moved))
    mz = z_pad(moved)
    rate_first = backward_diff(mx[0], nx, 0)
    rate_second = backward_diff(my[1], ny, 1)
    rate_third = backward_diff(mz[2], nz, 2)
    shear_one = forward_diff(my[0], ny, 1) + forward_diff(mx[1], nx, 0)
    shear_two = forward_diff(mz[0], nz, 2) + forward_diff(mx[2], nx, 0)
    shear_three = forward_diff(mz[1], nz, 2) + forward_diff(my[2], ny, 1)
    dilation = rate_first + rate_second + rate_third
    grown = stress + time_step * jnp.stack(
        [
            lame_first * dilation + 2.0 * shear_modulus * rate_first,
            lame_first * dilation + 2.0 * shear_modulus * rate_second,
            lame_first * dilation + 2.0 * shear_modulus * rate_third,
            shear_modulus * shear_one,
            shear_modulus * shear_two,
            shear_modulus * shear_three,
        ]
    )
    strain_vals = strain_now.astype(jnp.float32)
    lame_kernel = lame_kernel + time_step * (strain_vals[0] + strain_vals[1] + strain_vals[2]) * dilation
    shear_kernel = shear_kernel + 2.0 * time_step * (
        strain_vals[0] * rate_first
        + strain_vals[1] * rate_second
        + strain_vals[2] * rate_third
        + strain_vals[3] * shear_one
        + strain_vals[4] * shear_two
        + strain_vals[5] * shear_three
    )
    return (moved, grown, lame_kernel, shear_kernel)


def pair_kernel(block, samples, station_ref, mine_ref, other_ref, out_ref, acc_ref, toward_ref):
    step = pl.program_id(0)

    @pl.when(step == 0)
    def _():
        acc_ref[...] = jnp.zeros_like(acc_ref)

    mine_vals = mine_ref[...].astype(jnp.float32)
    other_vals = other_ref[...].astype(jnp.float32)
    mine_sq = jnp.sum(jnp.sum(mine_vals * mine_vals, axis=1, keepdims=True), axis=2, keepdims=True)
    other_sq = jnp.sum(jnp.sum(other_vals * other_vals, axis=1, keepdims=True), axis=2, keepdims=True)
    cross = jnp.sum(jnp.sum(mine_vals * other_vals, axis=1, keepdims=True), axis=2, keepdims=True)
    mine_norm = jnp.sqrt(mine_sq / samples + epsilon)
    other_norm = jnp.sqrt(other_sq / samples + epsilon)
    corr = (cross / samples) / (mine_norm * other_norm)
    toward = other_vals / other_norm - corr * (mine_vals / mine_norm)
    toward_ref[...] = toward.astype(jnp.bfloat16).astype(jnp.float32)

    ways = acc_ref.shape[0]

    def add_some(i, carry):
        for way in range(ways):
            slot = i * ways + way
            target = station_ref[step * block + slot]
            acc_ref[way, target] = acc_ref[way, target] + toward_ref[slot]
        return carry

    lax.fori_loop(0, block // ways, add_some, 0)

    @pl.when(step == pl.num_programs(0) - 1)
    def _():
        stations = out_ref.shape[0]
        total = acc_ref[0, :stations]
        for way in range(1, ways):
            total = total + acc_ref[way, :stations]
        out_ref[...] = total


def pair_sums(targets, mine, other, stations):
    slots, rows, lanes = mine.shape
    block = 64
    samples = rows * lanes
    spec = pl.BlockSpec((block, rows, lanes), lambda g, t: (g, 0, 0))
    return pl.pallas_call(
        functools.partial(pair_kernel, block, float(samples)),
        grid_spec=pltpu.PrefetchScalarGridSpec(
            num_scalar_prefetch=1,
            grid=(slots // block,),
            in_specs=[spec, spec],
            out_specs=pl.BlockSpec((stations, rows, lanes), lambda g, t: (0, 0, 0)),
            scratch_shapes=[
                pltpu.VMEM((4, stations + 1, rows, lanes), jnp.float32),
                pltpu.VMEM((block, rows, lanes), jnp.float32),
            ],
        ),
        out_shape=jax.ShapeDtypeStruct((stations, rows, lanes), jnp.float32),
        compiler_params=pltpu.CompilerParams(dimension_semantics=("arbitrary",)),
        cost_estimate=pl.CostEstimate(flops=20 * slots * samples, transcendentals=0, bytes_accessed=4 * slots * samples),
    )(targets, mine, other)


def station_part(residuals, station_cell, station_pairs, cells_first, cells_second, step_count):
    stations_here = residuals.shape[0]
    samples = residuals.shape[1]
    devices = lax.axis_size(("gx", "gy"))
    pair_rows = station_pairs.shape[0] // devices
    me = lax.axis_index(("gx", "gy"))
    own = lax.dynamic_slice_in_dim(station_pairs, me * pair_rows, pair_rows, 0)
    first_local = own[:, 0] - me * stations_here
    dest = own[:, 1] // stations_here
    order = jnp.arange(pair_rows)
    same = (dest[:, None] == dest[None, :]) & (order[None, :] < order[:, None])
    rank = jnp.sum(same.astype(jnp.int32), axis=1)
    device_ids = jnp.arange(devices)
    pick_own = (dest[None, :, None] == device_ids[:, None, None]) & (rank[None, :, None] == jnp.arange(2)[None, None, :])
    own_station = jnp.sum(jnp.where(pick_own, first_local[None, :, None] + 1, 0), axis=1) - 1
    blocks = station_pairs.reshape(devices, pair_rows, 2)
    hit = (blocks[:, :, 1] // stations_here == me).astype(jnp.int32)
    before = jnp.cumsum(hit, axis=1) - hit
    pick_in = (hit[:, :, None] > 0) & (before[:, :, None] == jnp.arange(2)[None, None, :])
    in_station = jnp.sum(jnp.where(pick_in, (blocks[:, :, 1] % stations_here)[:, :, None] + 1, 0), axis=1) - 1
    slot_station = jnp.concatenate([own_station, in_station], axis=1)
    lanes = 128
    rows = residuals.reshape(stations_here, samples // lanes, lanes)
    padded_rows = jnp.concatenate([rows, jnp.zeros((1,) + rows.shape[1:], rows.dtype)], axis=0)
    send = padded_rows[jnp.where(slot_station >= 0, slot_station, stations_here)]
    recv = lax.all_to_all(send, ("gx", "gy"), split_axis=0, concat_axis=0, tiled=True)
    mine_station = jnp.concatenate([slot_station[:, 2:4], slot_station[:, 0:2]], axis=1)
    mine = padded_rows[jnp.where(mine_station >= 0, mine_station, stations_here)]
    slots = devices * 4
    targets = jnp.where(mine_station >= 0, mine_station, stations_here).reshape(slots)
    adjoint3 = pair_sums(
        targets, mine.reshape(slots, samples // lanes, lanes), recv.reshape(slots, samples // lanes, lanes), stations_here
    )
    adjoint = adjoint3.reshape(stations_here, samples)
    last = adjoint3[:, samples // lanes - 1, lanes - step_count :]
    tail = last
    cells_hit = (station_cell[:, None] == jnp.arange(cells_first * cells_second)[None, :]).astype(jnp.float32)
    surfaces = jnp.stack(
        [
            jnp.sum(cells_hit * tail[:, step_count - 1 - window_step][:, None], axis=0).reshape(cells_first, cells_second)
            for window_step in range(step_count)
        ]
    )
    return adjoint, surfaces


def shards(velocity, stress, lame_first, shear_modulus, buoyancy, forward_strain, lame_accum, shear_accum, residuals, station_cell, station_pairs):
    step_count = forward_strain.shape[0] // 6
    adjoint, surfaces = station_part(residuals, station_cell, station_pairs, velocity.shape[1], velocity.shape[2], step_count)
    for window_step in range(step_count):
        strain_now = forward_strain[6 * window_step : 6 * window_step + 6]
        velocity, stress, lame_accum, shear_accum = advance(
            velocity, stress, lame_first, shear_modulus, buoyancy, strain_now, surfaces[window_step], lame_accum, shear_accum
        )
    return (velocity, stress, lame_accum, shear_accum, adjoint)


def solution(mesh):
    return jax.shard_map(
        shards,
        mesh=mesh,
        in_specs=(
            P(None, "gx", "gy", None),
            P(None, "gx", "gy", None),
            P("gx", "gy", None),
            P("gx", "gy", None),
            P("gx", "gy", None),
            P(None, "gx", "gy", None),
            P("gx", "gy", None),
            P("gx", "gy", None),
            P(("gx", "gy"), None),
            P(("gx", "gy")),
            P(),
        ),
        out_specs=(
            P(None, "gx", "gy", None),
            P(None, "gx", "gy", None),
            P("gx", "gy", None),
            P("gx", "gy", None),
            P(("gx", "gy"), None),
        ),
        check_vma=False,
    )
```

```python
import functools

import jax
import jax.numpy as jnp
from jax import lax
from jax.sharding import PartitionSpec as P
from jax.experimental import pallas as pl
from jax.experimental.pallas import tpu as pltpu

near_weight = 9.0 / 8.0
far_weight = -1.0 / 24.0
time_step = 0.25
epsilon = 1e-06


def shifted(padded, start, length, axis):
    return lax.slice_in_dim(padded, start, start + length, axis=axis)


def backward_diff(padded, length, axis):
    return near_weight * (
        shifted(padded, 2, length, axis) - shifted(padded, 1, length, axis)
    ) + far_weight * (shifted(padded, 3, length, axis) - shifted(padded, 0, length, axis))


def forward_diff(padded, length, axis):
    return near_weight * (
        shifted(padded, 3, length, axis) - shifted(padded, 2, length, axis)
    ) + far_weight * (shifted(padded, 4, length, axis) - shifted(padded, 1, length, axis))


def halo_pad(block, axis, dim, width=2):
    count = lax.axis_size(axis)
    forward = [(i, i + 1) for i in range(count - 1)]
    backward = [(i + 1, i) for i in range(count - 1)]
    size = block.shape[dim]
    low = lax.ppermute(lax.slice_in_dim(block, size - width, size, axis=dim), axis, forward)
    high = lax.ppermute(lax.slice_in_dim(block, 0, width, axis=dim), axis, backward)
    return jnp.concatenate([low, block, high], axis=dim)


def z_pad(block):
    pads = [(0, 0)] * (block.ndim - 1) + [(2, 2)]
    return jnp.pad(block, pads)


def exchange(block):
    wide_x = halo_pad(block[0], "gx", 1)
    wide_y = halo_pad(block[1], "gy", 2)
    return wide_x, wide_y


def advance(velocity, stress, lame_first, shear_modulus, buoyancy, strain_now, surface, lame_kernel, shear_kernel):
    nx = velocity.shape[1]
    ny = velocity.shape[2]
    nz = velocity.shape[3]
    sx, sy = exchange((jnp.stack([stress[0], stress[3], stress[4]]), jnp.stack([stress[3], stress[1], stress[5]])))
    sz = z_pad(jnp.stack([stress[4], stress[5], stress[2]]))
    force_first = forward_diff(sx[0], nx, 0) + backward_diff(sy[0], ny, 1) + backward_diff(sz[0], nz, 2)
    force_second = backward_diff(sx[1], nx, 0) + forward_diff(sy[1], ny, 1) + backward_diff(sz[1], nz, 2)
    force_third = backward_diff(sx[2], nx, 0) + backward_diff(sy[2], ny, 1) + forward_diff(sz[2], nz, 2)
    force_third = force_third.at[:, :, 0].add(surface)
    moved = velocity + time_step * buoyancy[None] * jnp.stack([force_first, force_second, force_third])
    mx, my = exchange((moved, moved))
    mz = z_pad(moved)
    rate_first = backward_diff(mx[0], nx, 0)
    rate_second = backward_diff(my[1], ny, 1)
    rate_third = backward_diff(mz[2], nz, 2)
    shear_one = forward_diff(my[0], ny, 1) + forward_diff(mx[1], nx, 0)
    shear_two = forward_diff(mz[0], nz, 2) + forward_diff(mx[2], nx, 0)
    shear_three = forward_diff(mz[1], nz, 2) + forward_diff(my[2], ny, 1)
    dilation = rate_first + rate_second + rate_third
    grown = stress + time_step * jnp.stack(
        [
            lame_first * dilation + 2.0 * shear_modulus * rate_first,
            lame_first * dilation + 2.0 * shear_modulus * rate_second,
            lame_first * dilation + 2.0 * shear_modulus * rate_third,
            shear_modulus * shear_one,
            shear_modulus * shear_two,
            shear_modulus * shear_three,
        ]
    )
    strain_vals = strain_now.astype(jnp.float32)
    lame_kernel = lame_kernel + time_step * (strain_vals[0] + strain_vals[1] + strain_vals[2]) * dilation
    shear_kernel = shear_kernel + 2.0 * time_step * (
        strain_vals[0] * rate_first
        + strain_vals[1] * rate_second
        + strain_vals[2] * rate_third
        + strain_vals[3] * shear_one
        + strain_vals[4] * shear_two
        + strain_vals[5] * shear_three
    )
    return (moved, grown, lame_kernel, shear_kernel)


def pair_kernel(block, samples, station_ref, mine_ref, other_ref, out_ref, acc_ref, toward_ref):
    step = pl.program_id(0)

    @pl.when(step == 0)
    def _():
        acc_ref[...] = jnp.zeros_like(acc_ref)

    mine_vals = mine_ref[...].astype(jnp.float32)
    other_vals = other_ref[...].astype(jnp.float32)
    mine_sq = jnp.sum(jnp.sum(mine_vals * mine_vals, axis=1, keepdims=True), axis=2, keepdims=True)
    other_sq = jnp.sum(jnp.sum(other_vals * other_vals, axis=1, keepdims=True), axis=2, keepdims=True)
    cross = jnp.sum(jnp.sum(mine_vals * other_vals, axis=1, keepdims=True), axis=2, keepdims=True)
    mine_norm = jnp.sqrt(mine_sq / samples + epsilon)
    other_norm = jnp.sqrt(other_sq / samples + epsilon)
    corr = (cross / samples) / (mine_norm * other_norm)
    toward = other_vals / other_norm - corr * (mine_vals / mine_norm)
    toward_ref[...] = toward.astype(jnp.bfloat16).astype(jnp.float32)

    ways = acc_ref.shape[0]

    def add_some(i, carry):
        for way in range(ways):
            slot = i * ways + way
            target = station_ref[step * block + slot]
            acc_ref[way, target] = acc_ref[way, target] + toward_ref[slot]
        return carry

    lax.fori_loop(0, block // ways, add_some, 0)

    @pl.when(step == pl.num_programs(0) - 1)
    def _():
        stations = out_ref.shape[0]
        total = acc_ref[0, :stations]
        for way in range(1, ways):
            total = total + acc_ref[way, :stations]
        out_ref[...] = total


def pair_sums(targets, mine, other, stations):
    slots, rows, lanes = mine.shape
    block = 64
    samples = rows * lanes
    spec = pl.BlockSpec((block, rows, lanes), lambda g, t: (g, 0, 0))
    return pl.pallas_call(
        functools.partial(pair_kernel, block, float(samples)),
        grid_spec=pltpu.PrefetchScalarGridSpec(
            num_scalar_prefetch=1,
            grid=(slots // block,),
            in_specs=[spec, spec],
            out_specs=pl.BlockSpec((stations, rows, lanes), lambda g, t: (0, 0, 0)),
            scratch_shapes=[
                pltpu.VMEM((4, stations + 1, rows, lanes), jnp.float32),
                pltpu.VMEM((block, rows, lanes), jnp.float32),
            ],
        ),
        out_shape=jax.ShapeDtypeStruct((stations, rows, lanes), jnp.float32),
        compiler_params=pltpu.CompilerParams(dimension_semantics=("arbitrary",)),
        cost_estimate=pl.CostEstimate(flops=20 * slots * samples, transcendentals=0, bytes_accessed=4 * slots * samples),
    )(targets, mine, other)


def station_part(residuals, station_cell, station_pairs, cells_first, cells_second, step_count):
    stations_here = residuals.shape[0]
    samples = residuals.shape[1]
    devices = lax.axis_size(("gx", "gy"))
    pair_rows = station_pairs.shape[0] // devices
    me = lax.axis_index(("gx", "gy"))
    own = lax.dynamic_slice_in_dim(station_pairs, me * pair_rows, pair_rows, 0)
    first_local = own[:, 0] - me * stations_here
    dest = own[:, 1] // stations_here
    order = jnp.arange(pair_rows)
    same = (dest[:, None] == dest[None, :]) & (order[None, :] < order[:, None])
    rank = jnp.sum(same.astype(jnp.int32), axis=1)
    device_ids = jnp.arange(devices)
    pick_own = (dest[None, :, None] == device_ids[:, None, None]) & (rank[None, :, None] == jnp.arange(2)[None, None, :])
    own_station = jnp.sum(jnp.where(pick_own, first_local[None, :, None] + 1, 0), axis=1) - 1
    seconds = station_pairs[:, 1].reshape(devices, pair_rows)
    hit = (seconds // stations_here == me).astype(jnp.int32)
    before = jnp.cumsum(hit, axis=1) - hit
    pick_in = (hit[:, :, None] > 0) & (before[:, :, None] == jnp.arange(2)[None, None, :])
    in_station = jnp.sum(jnp.where(pick_in, (seconds % stations_here)[:, :, None] + 1, 0), axis=1) - 1
    slot_station = jnp.concatenate([own_station, in_station], axis=1)
    lanes = 128
    rows = residuals.reshape(stations_here, samples // lanes, lanes)
    padded_rows = jnp.concatenate([rows, jnp.zeros((1,) + rows.shape[1:], rows.dtype)], axis=0)
    send = padded_rows[jnp.where(slot_station >= 0, slot_station, stations_here)]
    recv = lax.all_to_all(send, ("gx", "gy"), split_axis=0, concat_axis=0, tiled=True)
    mine_station = jnp.concatenate([slot_station[:, 2:4], slot_station[:, 0:2]], axis=1)
    mine = padded_rows[jnp.where(mine_station >= 0, mine_station, stations_here)]
    slots = devices * 4
    targets = jnp.where(mine_station >= 0, mine_station, stations_here).reshape(slots)
    adjoint3 = pair_sums(
        targets, mine.reshape(slots, samples // lanes, lanes), recv.reshape(slots, samples // lanes, lanes), stations_here
    )
    adjoint = adjoint3.reshape(stations_here, samples)
    last = adjoint3[:, samples // lanes - 1, lanes - step_count :]
    tail = last
    cells_hit = (station_cell[:, None] == jnp.arange(cells_first * cells_second)[None, :]).astype(jnp.float32)
    surfaces = jnp.stack(
        [
            jnp.sum(cells_hit * tail[:, step_count - 1 - window_step][:, None], axis=0).reshape(cells_first, cells_second)
            for window_step in range(step_count)
        ]
    )
    return adjoint, surfaces


def shards(velocity, stress, lame_first, shear_modulus, buoyancy, forward_strain, lame_accum, shear_accum, residuals, station_cell, station_pairs):
    step_count = forward_strain.shape[0] // 6
    adjoint, surfaces = station_part(residuals, station_cell, station_pairs, velocity.shape[1], velocity.shape[2], step_count)
    for window_step in range(step_count):
        strain_now = forward_strain[6 * window_step : 6 * window_step + 6]
        velocity, stress, lame_accum, shear_accum = advance(
            velocity, stress, lame_first, shear_modulus, buoyancy, strain_now, surfaces[window_step], lame_accum, shear_accum
        )
    return (velocity, stress, lame_accum, shear_accum, adjoint)


def solution(mesh):
    return jax.shard_map(
        shards,
        mesh=mesh,
        in_specs=(
            P(None, "gx", "gy", None),
            P(None, "gx", "gy", None),
            P("gx", "gy", None),
            P("gx", "gy", None),
            P("gx", "gy", None),
            P(None, "gx", "gy", None),
            P("gx", "gy", None),
            P("gx", "gy", None),
            P(("gx", "gy"), None),
            P(("gx", "gy")),
            P(),
        ),
        out_specs=(
            P(None, "gx", "gy", None),
            P(None, "gx", "gy", None),
            P("gx", "gy", None),
            P("gx", "gy", None),
            P(("gx", "gy"), None),
        ),
        check_vma=False,
    )
```
